256 devices in a mesh: ctx: 32 (over y, x, core), tp: 8 (over z).
Axes of the slice: x: 4, y: 4, z: 8, core: 2. Of those that a mesh axis runs over, the one named last changes fastest.
Arguments:
- queries: bfloat16 [24576, 8192], P('ctx', 'tp'), may hold values from -6 to 6
- keys: bfloat16 [24576, 8192], P('ctx', 'tp'), may hold values from -6 to 6
- values: bfloat16 [24576, 8192], P('ctx', 'tp'), may hold values from -40 to 40
- out_grad: bfloat16 [24576, 8192], P('ctx', 'tp'), may hold values from -6 to 6
- gain: float32 [8192], P('tp'), may hold values from 0.1 to 1.9
- doc_ids: int32 [24576], P('ctx'), may hold values from 0 to 7, never falling along the last dimension, each value on 1 to 12288 neighbouring positions
Outputs:
- normed: bfloat16 [24576, 8192], P('ctx', 'tp')
- grad_query: bfloat16 [24576, 8192], P('ctx', 'tp')
- grad_key: bfloat16 [24576, 8192], P('ctx', 'tp')
- grad_value: bfloat16 [24576, 8192], P('ctx', 'tp')
The draws below stay inside these ranges and needn't reach their ends.
Inputs may be any that keep to these rules, and one draw needn't show every extreme that they name: doc_ids never fall along the sequence; every one of the 8 documents has 1 to 12288 tokens and one has exactly 12288.
All inputs are finite; a program needn't handle non-finite values.
Results may differ from the reference program's by a relative error of at most 0.0062.
Values may be sent and summed in bfloat16 or wider, within the bound.
No kernel may reach another device: no remote copies, remote signals or barrier semaphores. Data moves between devices by JAX's collectives and lax.ppermute only.
A program may use at most 128 MiB of HBM per device.

```python
import math
import jax
import jax.numpy as jnp
import numpy as np
from jax import lax

HEADS = 64
HD = 128
TOK_DEV = 768
TOKENS = 24576
DOCS = 8
DOC_MOST = 12288
N_CTX = 32


def draw_values(key, part):
    key_base, key_column, key_row = jax.random.split(key, 3)
    column = jnp.arange(HEADS * HD)
    head_rise = 3.0 ** ((column // HD).astype(jnp.float32) / (HEADS - 1))
    column_scale = jnp.exp(jax.random.uniform(key_column, (HEADS * HD,), jnp.float32, 0.0, 2.302585))
    row_scale = jnp.exp(jax.random.uniform(key_row, (TOKENS, 1), jnp.float32, 0.0, 2.302585))
    base = jnp.clip(jax.random.normal(key_base, (TOKENS, HEADS * HD), jnp.float32), -4.0, 4.0)
    return (base * head_rise[None, :] * column_scale[None, :] * row_scale / 30.0).astype(jnp.bfloat16)


def level_of(rng, dims, cuts, least, high):
    loudness = 1.0
    for dim, shards_of in cuts:
        heights = jax.random.uniform(jax.random.fold_in(jax.random.fold_in(rng, 6), dim), (shards_of,), jnp.float32, least / len(cuts), high / len(cuts))
        loudness = loudness * jnp.repeat(jnp.exp(heights), dims[dim] // shards_of).reshape((-1,) + (1,) * (len(dims) - 1 - dim))
    return loudness


def profile(number_of, total, limit, lean):
    weights = [(1 << 20) // math.isqrt(standing ** lean) + 1 for standing in range(2, number_of + 1)]
    rest, counts = total - limit - (number_of - 1), [1] * (number_of - 1)
    while rest > 0:
        candidates = [i for i in range(number_of - 1) if counts[i] < limit]
        pool, budget = sum([weights[i] for i in candidates]), rest
        for i in candidates:
            more = min(limit - counts[i], max(1, budget * weights[i] // pool), rest)
            counts[i] = counts[i] + more
            rest = rest - more
    return np.array([limit] + counts)


def ragged(key, number_of, total, bound, skew):
    if number_of == 2:
        one = jax.random.randint(key, (), max(1, total - bound), min(bound, total - 1) + 1)
        return jnp.stack([one, total - one])
    tallies = jnp.asarray(profile(number_of, total, bound, skew), jnp.int32)
    pairs = (number_of - 1) // 2
    giver, receiver = tallies[1:1 + 2 * pairs:2], tallies[2:2 + 2 * pairs:2]
    slack = jnp.minimum(giver - 1, bound - receiver)
    passed = jax.random.randint(jax.random.fold_in(key, 1), (pairs,), 0, 1 << 20) % (slack + 1)
    tallies = tallies.at[1:1 + 2 * pairs:2].set(giver - passed).at[2:2 + 2 * pairs:2].set(receiver + passed)
    return tallies[jax.random.permutation(jax.random.fold_in(key, 2), number_of)]


def centred(stream_key, shape, spread, bound, cuts=(), kind=jnp.bfloat16):
    entries = jax.random.normal(stream_key, shape, jnp.float32) * spread
    if len(cuts) > 0:
        entries = level_of(stream_key, shape, cuts, -0.22, 0.18) * entries
    return jnp.clip(entries, min=-bound, max=bound).astype(kind)


def setup_inputs(seed: int = 0) -> dict:
    key_of = jax.random.split(jax.random.key(seed), 7)
    queries = centred(key_of[0], (TOKENS, HEADS * HD), 1.0, 6.0, ((0, 32), (1, 8)))
    keys = centred(key_of[1], (TOKENS, HEADS * HD), 1.0, 6.0, ((0, 32), (1, 8)))
    values = draw_values(jax.random.fold_in(key_of[6], 71), 0)
    out_grad = centred(key_of[3], (TOKENS, HEADS * HD), 1.0, 6.0, ((0, 32), (1, 8)))
    gain = jnp.clip(1.0 + 0.18 * jax.random.normal(key_of[4], (HEADS * HD,), jnp.float32), 0.1, 1.9)
    doc_ids = jnp.searchsorted(jnp.cumsum(ragged(key_of[5], DOCS, TOKENS, DOC_MOST, 1)), jnp.arange(TOKENS), side="right").astype(jnp.int32)
    return dict(queries=queries, keys=keys, values=values, out_grad=out_grad, gain=gain, doc_ids=doc_ids)


NORM_EPS = 1e-06

def product(form, left, right):
    return jnp.einsum(form, left.astype(jnp.float32), right.astype(jnp.float32))

def doc_mask_of(doc_block):
    position = jnp.arange(TOK_DEV)
    same_doc = doc_block[:, None] == doc_block[None, :]
    return (same_doc & (position[:, None] >= position[None, :])).astype(jnp.float32)

def reference(queries, keys, values, out_grad, gain, doc_ids):
    width = HEADS * HD
    query_blocks = queries.reshape(N_CTX, TOK_DEV, HEADS, HD)
    key_blocks = keys.reshape(N_CTX, TOK_DEV, HEADS, HD)
    value_blocks = values.reshape(N_CTX, TOK_DEV, HEADS, HD)
    grad_blocks = out_grad.reshape(N_CTX, TOK_DEV, width)
    doc_blocks = doc_ids.reshape(N_CTX, TOK_DEV)
    first_docs = doc_blocks[:, 0]
    last_docs = doc_blocks[:, TOK_DEV - 1]

    def forward_state(pieces):
        key_block, value_block, doc_block = pieces
        chosen = (doc_block == doc_block[TOK_DEV - 1]).astype(jnp.float32)
        return product('tha,thb->hab', key_block * chosen[:, None, None], value_block).astype(jnp.bfloat16)
    states = lax.map(forward_state, (key_blocks, value_blocks, doc_blocks))
    start_state = (jnp.zeros((HEADS, HD, HD), jnp.float32), jnp.int32(-1))

    def carry_forward(carried, pieces):
        running, running_doc = carried
        block_state, first_doc, last_doc = pieces
        arriving = jnp.where(running_doc == first_doc, running, 0.0).astype(jnp.bfloat16)
        running = jnp.where(running_doc == last_doc, running, 0.0) + block_state.astype(jnp.float32)
        return ((running, last_doc), arriving)
    _, incoming = lax.scan(carry_forward, start_state, (states, first_docs, last_docs))

    def middle(pieces):
        query_block, key_block, value_block, grad_block, doc_block, arriving = pieces
        doc_mask = doc_mask_of(doc_block)
        first_rows = (doc_block == doc_block[0]).astype(jnp.float32)[:, None, None]
        scores = (product('tha,sha->hts', query_block, key_block) * doc_mask[None]).astype(jnp.bfloat16)
        attended = product('hts,shb->thb', scores, value_block) + product('tha,hab->thb', query_block, arriving) * first_rows
        flat = attended.reshape(TOK_DEV, width)
        inverse = lax.rsqrt(lax.optimization_barrier(jnp.sum(flat * flat, axis=1)) / width + NORM_EPS)
        normed = (flat * inverse[:, None] * gain[None, :]).astype(jnp.bfloat16)
        scaled_grad = gain[None, :] * grad_block.astype(jnp.float32)
        cross_sum = lax.optimization_barrier(jnp.sum(scaled_grad * flat, axis=1))
        delta = (inverse[:, None] * scaled_grad - flat * (inverse ** 3 * cross_sum / width)[:, None]).astype(jnp.bfloat16)
        delta_rows = delta.reshape(TOK_DEV, HEADS, HD)
        reverse_state = product('tha,thb->hab', query_block * first_rows, delta_rows).astype(jnp.bfloat16)
        dscores = (product('thb,shb->hts', delta_rows, value_block) * doc_mask[None]).astype(jnp.bfloat16)
        grad_query = product('hts,sha->tha', dscores, key_block) + product('thb,hab->tha', delta_rows, arriving) * first_rows
        return (normed, grad_query.astype(jnp.bfloat16), delta_rows, reverse_state)
    normed, grad_query, deltas, reverse_states = lax.map(middle, (query_blocks, key_blocks, value_blocks, grad_blocks, doc_blocks, incoming))

    def carry_backward(carried, pieces):
        running, running_doc = carried
        block_state, first_doc, last_doc = pieces
        leaving = jnp.where(running_doc == last_doc, running, 0.0).astype(jnp.bfloat16)
        running = jnp.where(running_doc == first_doc, running, 0.0) + block_state.astype(jnp.float32)
        return ((running, first_doc), leaving)
    _, outgoing = lax.scan(carry_backward, start_state, (reverse_states, first_docs, last_docs), reverse=True)

    def finish(pieces):
        query_block, key_block, value_block, delta_rows, doc_block, leaving = pieces
        doc_mask = doc_mask_of(doc_block)
        last_rows = (doc_block == doc_block[TOK_DEV - 1]).astype(jnp.float32)[:, None, None]
        scores = (product('tha,sha->hts', query_block, key_block) * doc_mask[None]).astype(jnp.bfloat16)
        dscores = (product('thb,shb->hts', delta_rows, value_block) * doc_mask[None]).astype(jnp.bfloat16)
        grad_key = product('hts,tha->sha', dscores, query_block) + product('thb,hab->tha', value_block, leaving) * last_rows
        grad_value = product('hts,thb->shb', scores, delta_rows) + product('tha,hab->thb', key_block, leaving) * last_rows
        return (grad_key.astype(jnp.bfloat16), grad_value.astype(jnp.bfloat16))
    grad_key, grad_value = lax.map(finish, (query_blocks, key_blocks, value_blocks, deltas, doc_blocks, outgoing))
    return (normed.reshape(TOKENS, width), grad_query.reshape(TOKENS, width), grad_key.reshape(TOKENS, width), grad_value.reshape(TOKENS, width))
```

```python
import jax
import jax.numpy as jnp
from jax import lax
from jax.sharding import PartitionSpec as P

HEADS = 64
HD = 128


NORM_EPS = 1e-06


DOC_MOST = 12288


def moved(x, axis, count, by, backward):
    if backward:
        pairs = [(i, i - by) for i in range(by, count)]
    else:
        pairs = [(i, i + by) for i in range(count - by)]
    return lax.ppermute(x, axis, pairs)


def carried(state, first_tag, last_tag, tokens_here, axis, backward):
    count = lax.axis_size(axis)
    window = min((DOC_MOST - 1) // tokens_here + 1, count)
    link_tag = first_tag if backward else last_tag
    meet_tag = last_tag if backward else first_tag
    near_tag = moved(link_tag, axis, count, 1, backward)
    own_link = (near_tag == link_tag).astype(jnp.float32)
    own_meet = (near_tag == meet_tag).astype(jnp.float32)
    total = moved(state, axis, count, 1, backward).astype(jnp.float32)
    link = moved(own_link, axis, count, 1, backward)
    span = 1
    if window > 1:
        total = total + link * moved(state, axis, count, 2, backward).astype(jnp.float32)
        link = link * moved(own_link, axis, count, 2, backward)
        span = 2
    while span < window:
        far_total = moved(total, axis, count, span, backward)
        far_link = moved(link, axis, count, span, backward)
        total = total + link * far_total
        link = link * far_link
        span = span * 2
    return (own_meet * total).astype(jnp.bfloat16)


def shards(queries, keys, values, out_grad, gain, doc_ids):
    tokens_here = queries.shape[0]
    heads_here = queries.shape[1] // HD
    width_all = HEADS * HD
    flat_width = heads_here * HD
    query_heads = queries.reshape(tokens_here, heads_here, HD).transpose(1, 0, 2)
    key_heads = keys.reshape(tokens_here, heads_here, HD).transpose(1, 0, 2)
    value_heads = values.reshape(tokens_here, heads_here, HD).transpose(1, 0, 2)
    position = jnp.arange(tokens_here)
    doc_mask = (
        (doc_ids[:, None] == doc_ids[None, :]) & (position[:, None] >= position[None, :])
    ).astype(jnp.bfloat16)
    first_doc = doc_ids[0]
    last_doc = doc_ids[tokens_here - 1]
    first_rows = (doc_ids == first_doc).astype(jnp.bfloat16)[None, :, None]
    last_rows = (doc_ids == last_doc).astype(jnp.bfloat16)[None, :, None]
    zero_state = jnp.zeros((heads_here, HD, HD), jnp.float32)
    query_first = query_heads * first_rows
    key_last = key_heads * last_rows
    value_last = value_heads * last_rows
    own_state = jnp.einsum(
        "hta,htb->hab", key_last, value_heads, preferred_element_type=jnp.float32
    ).astype(jnp.bfloat16)
    first_tag = first_doc.astype(jnp.float32) + 1.0
    last_tag = last_doc.astype(jnp.float32) + 1.0
    incoming = carried(own_state, first_tag, last_tag, tokens_here, "ctx", False)
    scores = (
        jnp.einsum("hta,hsa->hts", query_heads, key_heads, preferred_element_type=jnp.float32)
        * doc_mask[None]
    ).astype(jnp.bfloat16)
    attended_heads = jnp.einsum(
        "htk,hkb->htb",
        jnp.concatenate([scores, query_first], axis=2),
        jnp.concatenate([value_heads, incoming], axis=1),
        preferred_element_type=jnp.float32,
    )
    flat = attended_heads.transpose(1, 0, 2).reshape(tokens_here, flat_width)
    scaled_grad = gain[None, :] * out_grad.astype(jnp.float32)
    square_sum, cross_sum = lax.psum(
        (jnp.sum(flat * flat, axis=1), jnp.sum(scaled_grad * flat, axis=1)), "tp"
    )
    inverse = lax.rsqrt(square_sum / width_all + NORM_EPS)
    normed = (flat * inverse[:, None] * gain[None, :]).astype(jnp.bfloat16)
    delta = (
        inverse[:, None] * scaled_grad - flat * (inverse**3 * cross_sum / width_all)[:, None]
    ).astype(jnp.bfloat16)
    delta_heads = delta.reshape(tokens_here, heads_here, HD).transpose(1, 0, 2)
    own_reverse = jnp.einsum(
        "hta,htb->hab", query_first, delta_heads, preferred_element_type=jnp.float32
    ).astype(jnp.bfloat16)
    outgoing = carried(own_reverse, first_tag, last_tag, tokens_here, "ctx", True)
    dscores = (
        jnp.einsum("htb,hsb->hts", delta_heads, value_heads, preferred_element_type=jnp.float32)
        * doc_mask[None]
    ).astype(jnp.bfloat16)
    grad_query = jnp.einsum(
        "htk,hka->hta",
        jnp.concatenate([dscores, delta_heads * first_rows], axis=2),
        jnp.concatenate([key_heads, incoming.transpose(0, 2, 1)], axis=1),
        preferred_element_type=jnp.float32,
    )
    grad_key = jnp.einsum(
        "hks,hka->hsa",
        jnp.concatenate([dscores, value_last.transpose(0, 2, 1)], axis=1),
        jnp.concatenate([query_heads, outgoing.transpose(0, 2, 1)], axis=1),
        preferred_element_type=jnp.float32,
    )
    grad_value = jnp.einsum(
        "hks,hkb->hsb",
        jnp.concatenate([scores, key_last.transpose(0, 2, 1)], axis=1),
        jnp.concatenate([delta_heads, outgoing], axis=1),
        preferred_element_type=jnp.float32,
    )
    return (
        normed,
        grad_query.astype(jnp.bfloat16).transpose(1, 0, 2).reshape(tokens_here, flat_width),
        grad_key.astype(jnp.bfloat16).transpose(1, 0, 2).reshape(tokens_here, flat_width),
        grad_value.astype(jnp.bfloat16).transpose(1, 0, 2).reshape(tokens_here, flat_width),
    )


def solution(mesh):
    in_specs = (P("ctx", "tp"), P("ctx", "tp"), P("ctx", "tp"), P("ctx", "tp"), P("tp"), P("ctx"))
    out_specs = (P("ctx", "tp"), P("ctx", "tp"), P("ctx", "tp"), P("ctx", "tp"))
    return jax.shard_map(shards, mesh=mesh, in_specs=in_specs, out_specs=out_specs, check_vma=False)
```

```python
import jax
import jax.numpy as jnp
from jax import lax
from jax.sharding import PartitionSpec as P

HEADS = 64
HD = 128
DOC_MOST = 12288

NORM_EPS = 1e-06


def moved(x, axis, count, by, backward):
    if backward:
        pairs = [(i, i - by) for i in range(by, count)]
    else:
        pairs = [(i, i + by) for i in range(count - by)]
    return lax.ppermute(x, axis, pairs)


def swapped(x, axis, count):
    return lax.ppermute(x, axis, [(i, i ^ 1) for i in range(count)])


def carried(state, firsts, lasts, tokens_here, axis, backward, partial_type):
    count = lax.axis_size(axis)
    index = lax.axis_index(axis)
    if backward:
        link_tags, meet_tags, place = firsts[::-1], lasts[::-1], count - 1 - index
    else:
        link_tags, meet_tags, place = lasts, firsts, index
    earlier = jnp.concatenate([jnp.full((1,), -1.0, jnp.float32), link_tags[:-1]])
    links = (earlier == link_tags).astype(jnp.float32)
    meets = (earlier == meet_tags).astype(jnp.float32)
    chips = count // 2
    terms = min((DOC_MOST - 1) // tokens_here + 1, count)
    window = min((terms + 1) // 2, chips)
    chip_links = links[0::2] * links[1::2]
    padded_links = jnp.concatenate([jnp.zeros((window,), jnp.float32), chip_links])
    chip = place // 2
    core = place % 2
    half = state.shape[0] // 2
    own_half = lax.dynamic_slice_in_dim(state, core * half, half, 0)
    other_half = lax.dynamic_slice_in_dim(state, (1 - core) * half, half, 0)
    partner_half = swapped(other_half, axis, count)
    low = jnp.where(core == 0, own_half, partner_half).astype(jnp.float32)
    high = jnp.where(core == 0, partner_half, own_half).astype(jnp.float32)
    chip_total = high + links[2 * chip + 1] * low
    total = moved(chip_total, axis, count, 2, backward)
    span = 1
    while span < window:
        reach = jnp.prod(lax.dynamic_slice_in_dim(padded_links, chip + window - span, span, 0))
        far = moved(total.astype(partial_type), axis, count, 2 * span, backward)
        total = total + reach * far.astype(jnp.float32)
        span = span * 2
    out_low = meets[2 * chip] * total
    out_high = meets[2 * chip + 1] * (low + links[2 * chip] * total)
    mine = jnp.where(core == 0, out_low, out_high).astype(jnp.bfloat16)
    theirs = jnp.where(core == 0, out_high, out_low).astype(jnp.bfloat16)
    got = swapped(theirs, axis, count)
    return jnp.where(
        core == 0, jnp.concatenate([mine, got], axis=0), jnp.concatenate([got, mine], axis=0)
    )


def group_sum(x, axis):
    count = lax.axis_size(axis)
    step = 1
    while step < count:
        x = x + lax.ppermute(x, axis, [(i, i ^ step) for i in range(count)])
        step = step * 2
    return x


def shards(queries, keys, values, out_grad, gain, doc_ids):
    tokens_here = queries.shape[0]
    heads_here = queries.shape[1] // HD
    width_all = HEADS * HD
    flat_width = heads_here * HD
    query_heads = queries.reshape(tokens_here, heads_here, HD).transpose(1, 0, 2)
    key_heads = keys.reshape(tokens_here, heads_here, HD).transpose(1, 0, 2)
    value_heads = values.reshape(tokens_here, heads_here, HD).transpose(1, 0, 2)
    position = jnp.arange(tokens_here)
    doc_mask = (
        (doc_ids[:, None] == doc_ids[None, :]) & (position[:, None] >= position[None, :])
    ).astype(jnp.bfloat16)
    first_doc = doc_ids[0]
    last_doc = doc_ids[tokens_here - 1]
    ends = lax.all_gather(
        jnp.stack([first_doc, last_doc]).astype(jnp.float32) + 1.0, "ctx"
    )
    firsts, lasts = ends[:, 0], ends[:, 1]
    first_rows = (doc_ids == first_doc).astype(jnp.bfloat16)[None, :, None]
    last_rows = (doc_ids == last_doc).astype(jnp.bfloat16)[None, :, None]
    query_first = query_heads * first_rows
    key_last = key_heads * last_rows
    value_last = value_heads * last_rows
    own_state = jnp.einsum(
        "hta,htb->hab", key_last, value_heads, preferred_element_type=jnp.float32
    ).astype(jnp.bfloat16)
    incoming = carried(own_state, firsts, lasts, tokens_here, "ctx", False, jnp.bfloat16)
    scores = (
        jnp.einsum("hta,hsa->hts", query_heads, key_heads, preferred_element_type=jnp.float32)
        * doc_mask[None]
    ).astype(jnp.bfloat16)
    attended_heads = jnp.einsum(
        "hts,hsb->htb", scores, value_heads, preferred_element_type=jnp.float32
    ) + jnp.einsum("hta,hab->htb", query_first, incoming, preferred_element_type=jnp.float32)
    flat = attended_heads.transpose(1, 0, 2).reshape(tokens_here, flat_width)
    scaled_grad = gain[None, :] * out_grad.astype(jnp.float32)
    sums = group_sum(
        jnp.stack([jnp.sum(flat * flat, axis=1), jnp.sum(scaled_grad * flat, axis=1)]), "tp"
    )
    square_sum, cross_sum = sums[0], sums[1]
    inverse = lax.rsqrt(square_sum / width_all + NORM_EPS)
    normed = (flat * inverse[:, None] * gain[None, :]).astype(jnp.bfloat16)
    delta = (
        inverse[:, None] * scaled_grad - flat * (inverse**3 * cross_sum / width_all)[:, None]
    ).astype(jnp.bfloat16)
    delta_heads = delta.reshape(tokens_here, heads_here, HD).transpose(1, 0, 2)
    own_reverse = jnp.einsum(
        "hta,htb->hab", query_first, delta_heads, preferred_element_type=jnp.float32
    ).astype(jnp.bfloat16)
    outgoing = carried(own_reverse, firsts, lasts, tokens_here, "ctx", True, jnp.bfloat16)
    dscores = (
        jnp.einsum("htb,hsb->hts", delta_heads, value_heads, preferred_element_type=jnp.float32)
        * doc_mask[None]
    ).astype(jnp.bfloat16)
    grad_query = jnp.einsum(
        "hts,hsa->hta", dscores, key_heads, preferred_element_type=jnp.float32
    ) + jnp.einsum(
        "htb,hab->hta", delta_heads * first_rows, incoming, preferred_element_type=jnp.float32
    )
    grad_key = jnp.einsum(
        "hts,hta->hsa", dscores, query_heads, preferred_element_type=jnp.float32
    ) + jnp.einsum("hsb,hab->hsa", value_last, outgoing, preferred_element_type=jnp.float32)
    grad_value = jnp.einsum(
        "hts,htb->hsb", scores, delta_heads, preferred_element_type=jnp.float32
    ) + jnp.einsum("hsa,hab->hsb", key_last, outgoing, preferred_element_type=jnp.float32)
    return (
        normed,
        grad_query.astype(jnp.bfloat16).transpose(1, 0, 2).reshape(tokens_here, flat_width),
        grad_key.astype(jnp.bfloat16).transpose(1, 0, 2).reshape(tokens_here, flat_width),
        grad_value.astype(jnp.bfloat16).transpose(1, 0, 2).reshape(tokens_here, flat_width),
    )


def solution(mesh):
    in_specs = (P("ctx", "tp"), P("ctx", "tp"), P("ctx", "tp"), P("ctx", "tp"), P("tp"), P("ctx"))
    out_specs = (P("ctx", "tp"), P("ctx", "tp"), P("ctx", "tp"), P("ctx", "tp"))
    return jax.shard_map(shards, mesh=mesh, in_specs=in_specs, out_specs=out_specs, check_vma=False)
```

```python
import jax
import jax.numpy as jnp
from jax import lax
from jax.sharding import PartitionSpec as P

HEADS = 64
HD = 128
DOC_MOST = 12288

NORM_EPS = 1e-06


def moved(x, axis, count, by, backward):
    if backward:
        pairs = [(i, i - by) for i in range(by, count)]
    else:
        pairs = [(i, i + by) for i in range(count - by)]
    return lax.ppermute(x, axis, pairs)


def swapped(x, axis, count):
    return lax.ppermute(x, axis, [(i, i ^ 1) for i in range(count)])


def packed(data, tags):
    rows = data.reshape(-1, data.shape[-1])
    tail = jnp.zeros((16, rows.shape[1]), data.dtype)
    tail = tail.at[0, : len(tags)].set(jnp.stack(tags).astype(data.dtype))
    return jnp.concatenate([rows, tail], axis=0)


def unpacked(message, shape):
    data = message[: message.shape[0] - 16].reshape(shape)
    return data, message[message.shape[0] - 16, :4].astype(jnp.float32)


def carried(state, first_tag, last_tag, tokens_here, axis, backward, partial_type):
    count = lax.axis_size(axis)
    index = lax.axis_index(axis)
    if backward:
        link_tag, meet_tag, place = first_tag, last_tag, count - 1 - index
    else:
        link_tag, meet_tag, place = last_tag, first_tag, index
    chips = count // 2
    terms = min((DOC_MOST - 1) // tokens_here + 1, count)
    window = min((terms + 1) // 2, chips)
    core = place % 2
    half = state.shape[0] // 2
    half_shape = (half,) + state.shape[1:]
    own_half = lax.dynamic_slice_in_dim(state, core * half, half, 0)
    other_half = lax.dynamic_slice_in_dim(state, (1 - core) * half, half, 0)
    partner_half, partner_tags = unpacked(
        swapped(packed(other_half, [link_tag, meet_tag]), axis, count), half_shape
    )
    first_core = core == 0
    low = jnp.where(first_core, own_half, partner_half).astype(jnp.float32)
    high = jnp.where(first_core, partner_half, own_half).astype(jnp.float32)
    low_link = jnp.where(first_core, link_tag, partner_tags[0])
    high_link = jnp.where(first_core, partner_tags[0], link_tag)
    low_meet = jnp.where(first_core, meet_tag, partner_tags[1])
    high_meet = jnp.where(first_core, partner_tags[1], meet_tag)
    chip_total = high + (low_link == high_link).astype(jnp.float32) * low
    total, near_tags = unpacked(
        moved(packed(chip_total, [high_link]), axis, count, 2, backward), half_shape
    )
    before = near_tags[0]
    span = 1
    while span < window:
        far, far_tags = unpacked(
            moved(packed(total.astype(partial_type), [before]), axis, count, 2 * span, backward),
            half_shape,
        )
        reach = (far_tags[0] == before).astype(jnp.float32)
        total = total + reach * far.astype(jnp.float32)
        span = span * 2
    out_low = (before == low_meet).astype(jnp.float32) * total
    out_high = (low_link == high_meet).astype(jnp.float32) * (
        low + (before == low_link).astype(jnp.float32) * total
    )
    mine = jnp.where(first_core, out_low, out_high).astype(jnp.bfloat16)
    theirs = jnp.where(first_core, out_high, out_low).astype(jnp.bfloat16)
    got = swapped(theirs, axis, count)
    return jnp.where(
        first_core, jnp.concatenate([mine, got], axis=0), jnp.concatenate([got, mine], axis=0)
    )


def group_sum(x, axis):
    count = lax.axis_size(axis)
    step = 1
    while step < count:
        x = x + lax.ppermute(x, axis, [(i, i ^ step) for i in range(count)])
        step = step * 2
    return x


def shards(queries, keys, values, out_grad, gain, doc_ids):
    tokens_here = queries.shape[0]
    heads_here = queries.shape[1] // HD
    width_all = HEADS * HD
    flat_width = heads_here * HD
    query_heads = queries.reshape(tokens_here, heads_here, HD).transpose(1, 0, 2)
    key_heads = keys.reshape(tokens_here, heads_here, HD).transpose(1, 0, 2)
    value_heads = values.reshape(tokens_here, heads_here, HD).transpose(1, 0, 2)
    position = jnp.arange(tokens_here)
    doc_mask = (
        (doc_ids[:, None] == doc_ids[None, :]) & (position[:, None] >= position[None, :])
    ).astype(jnp.bfloat16)
    first_doc = doc_ids[0]
    last_doc = doc_ids[tokens_here - 1]
    first_tag = first_doc.astype(jnp.float32) + 1.0
    last_tag = last_doc.astype(jnp.float32) + 1.0
    first_rows = (doc_ids == first_doc).astype(jnp.bfloat16)[None, :, None]
    last_rows = (doc_ids == last_doc).astype(jnp.bfloat16)[None, :, None]
    query_first = query_heads * first_rows
    key_last = key_heads * last_rows
    value_last = value_heads * last_rows
    own_state = jnp.einsum(
        "hta,htb->hab", key_last, value_heads, preferred_element_type=jnp.float32
    ).astype(jnp.bfloat16)
    incoming = carried(own_state, first_tag, last_tag, tokens_here, "ctx", False, jnp.bfloat16)
    scores = (
        jnp.einsum("hta,hsa->hts", query_heads, key_heads, preferred_element_type=jnp.float32)
        * doc_mask[None]
    ).astype(jnp.bfloat16)
    attended_heads = jnp.einsum(
        "hts,hsb->htb", scores, value_heads, preferred_element_type=jnp.float32
    ) + jnp.einsum("hta,hab->htb", query_first, incoming, preferred_element_type=jnp.float32)
    flat = attended_heads.transpose(1, 0, 2).reshape(tokens_here, flat_width)
    scaled_grad = gain[None, :] * out_grad.astype(jnp.float32)
    sums = group_sum(
        jnp.stack([jnp.sum(flat * flat, axis=1), jnp.sum(scaled_grad * flat, axis=1)]), "tp"
    )
    square_sum, cross_sum = sums[0], sums[1]
    inverse = lax.rsqrt(square_sum / width_all + NORM_EPS)
    normed = (flat * inverse[:, None] * gain[None, :]).astype(jnp.bfloat16)
    delta = (
        inverse[:, None] * scaled_grad - flat * (inverse**3 * cross_sum / width_all)[:, None]
    ).astype(jnp.bfloat16)
    delta_heads = delta.reshape(tokens_here, heads_here, HD).transpose(1, 0, 2)
    own_reverse = jnp.einsum(
        "hta,htb->hab", query_first, delta_heads, preferred_element_type=jnp.float32
    ).astype(jnp.bfloat16)
    outgoing = carried(own_reverse, first_tag, last_tag, tokens_here, "ctx", True, jnp.bfloat16)
    dscores = (
        jnp.einsum("htb,hsb->hts", delta_heads, value_heads, preferred_element_type=jnp.float32)
        * doc_mask[None]
    ).astype(jnp.bfloat16)
    grad_query = jnp.einsum(
        "hts,hsa->hta", dscores, key_heads, preferred_element_type=jnp.float32
    ) + jnp.einsum(
        "htb,hab->hta", delta_heads * first_rows, incoming, preferred_element_type=jnp.float32
    )
    grad_key = jnp.einsum(
        "hts,hta->hsa", dscores, query_heads, preferred_element_type=jnp.float32
    ) + jnp.einsum("hsb,hab->hsa", value_last, outgoing, preferred_element_type=jnp.float32)
    grad_value = jnp.einsum(
        "hts,htb->hsb", scores, delta_heads, preferred_element_type=jnp.float32
    ) + jnp.einsum("hsa,hab->hsb", key_last, outgoing, preferred_element_type=jnp.float32)
    return (
        normed,
        grad_query.astype(jnp.bfloat16).transpose(1, 0, 2).reshape(tokens_here, flat_width),
        grad_key.astype(jnp.bfloat16).transpose(1, 0, 2).reshape(tokens_here, flat_width),
        grad_value.astype(jnp.bfloat16).transpose(1, 0, 2).reshape(tokens_here, flat_width),
    )


def solution(mesh):
    in_specs = (P("ctx", "tp"), P("ctx", "tp"), P("ctx", "tp"), P("ctx", "tp"), P("tp"), P("ctx"))
    out_specs = (P("ctx", "tp"), P("ctx", "tp"), P("ctx", "tp"), P("ctx", "tp"))
    return jax.shard_map(shards, mesh=mesh, in_specs=in_specs, out_specs=out_specs, check_vma=False)
```

```python
import jax
import jax.numpy as jnp
from jax import lax
from jax.experimental import pallas as pl
from jax.sharding import PartitionSpec as P

HEADS = 64
HD = 128
DOC_MOST = 12288

NORM_EPS = 1e-06


def moved(x, axis, count, by, backward):
    if backward:
        pairs = [(i, i - by) for i in range(by, count)]
    else:
        pairs = [(i, i + by) for i in range(count - by)]
    return lax.ppermute(x, axis, pairs)


def swapped(x, axis, count):
    return lax.ppermute(x, axis, [(i, i ^ 1) for i in range(count)])


def packed(data, tags):
    rows = data.reshape(-1, data.shape[-1])
    tail = jnp.zeros((16, rows.shape[1]), data.dtype)
    tail = tail.at[0, : len(tags)].set(jnp.stack(tags).astype(data.dtype))
    return jnp.concatenate([rows, tail], axis=0)


def unpacked(message, shape):
    data = message[: message.shape[0] - 16].reshape(shape)
    return data, message[message.shape[0] - 16, :4].astype(jnp.float32)


def carried(state, first_tag, last_tag, tokens_here, axis, backward, partial_type):
    count = lax.axis_size(axis)
    index = lax.axis_index(axis)
    if backward:
        link_tag, meet_tag, place = first_tag, last_tag, count - 1 - index
    else:
        link_tag, meet_tag, place = last_tag, first_tag, index
    chips = count // 2
    terms = min((DOC_MOST - 1) // tokens_here + 1, count)
    window = min((terms + 1) // 2, chips)
    core = place % 2
    half = state.shape[0] // 2
    half_shape = (half,) + state.shape[1:]
    own_half = lax.dynamic_slice_in_dim(state, core * half, half, 0)
    other_half = lax.dynamic_slice_in_dim(state, (1 - core) * half, half, 0)
    partner_half, partner_tags = unpacked(
        swapped(packed(other_half, [link_tag, meet_tag]), axis, count), half_shape
    )
    first_core = core == 0
    low = jnp.where(first_core, own_half, partner_half).astype(jnp.float32)
    high = jnp.where(first_core, partner_half, own_half).astype(jnp.float32)
    low_link = jnp.where(first_core, link_tag, partner_tags[0])
    high_link = jnp.where(first_core, partner_tags[0], link_tag)
    low_meet = jnp.where(first_core, meet_tag, partner_tags[1])
    high_meet = jnp.where(first_core, partner_tags[1], meet_tag)
    chip_total = high + (low_link == high_link).astype(jnp.float32) * low
    total, near_tags = unpacked(
        moved(packed(chip_total, [high_link]), axis, count, 2, backward), half_shape
    )
    before = near_tags[0]
    span = 1
    while span < window:
        far, far_tags = unpacked(
            moved(packed(total.astype(partial_type), [before]), axis, count, 2 * span, backward),
            half_shape,
        )
        reach = (far_tags[0] == before).astype(jnp.float32)
        total = total + reach * far.astype(jnp.float32)
        span = span * 2
    out_low = (before == low_meet).astype(jnp.float32) * total
    out_high = (low_link == high_meet).astype(jnp.float32) * (
        low + (before == low_link).astype(jnp.float32) * total
    )
    mine = jnp.where(first_core, out_low, out_high).astype(jnp.bfloat16)
    theirs = jnp.where(first_core, out_high, out_low).astype(jnp.bfloat16)
    got = swapped(theirs, axis, count)
    return jnp.where(
        first_core, jnp.concatenate([mine, got], axis=0), jnp.concatenate([got, mine], axis=0)
    )


def group_sum(x, axis):
    count = lax.axis_size(axis)
    index = lax.axis_index(axis)
    parts = [x]
    for step in range(1, count):
        parts.append(lax.ppermute(x, axis, [(i, (i + step) % count) for i in range(count)]))
    ordered = jnp.stack(parts)
    slot = (index - jnp.arange(count)) % count
    ordered = ordered[slot]
    total = ordered[0]
    for source in range(1, count):
        total = total + ordered[source]
    return total


def finish_body(local_ref, rows_ref, mask_ref, state_ref, out_ref, *, flip):
    rows = rows_ref[...] * mask_ref[...]
    state = state_ref[0]
    if flip:
        extra = lax.dot_general(
            rows, state, (((1,), (1,)), ((), ())), preferred_element_type=jnp.float32
        )
    else:
        extra = jnp.dot(rows, state, preferred_element_type=jnp.float32)
    out_ref[...] = (local_ref[0] + extra).astype(out_ref.dtype)


def finished(local, rows, mask, state, flip, kind, interpret=False):
    heads, tokens, width = local.shape
    return pl.pallas_call(
        lambda *refs: finish_body(*refs, flip=flip),
        grid=(heads,),
        in_specs=[
            pl.BlockSpec((1, tokens, width), lambda h: (h, 0, 0)),
            pl.BlockSpec((tokens, width), lambda h: (0, h)),
            pl.BlockSpec((tokens, 1), lambda h: (0, 0)),
            pl.BlockSpec((1, width, width), lambda h: (h, 0, 0)),
        ],
        out_specs=pl.BlockSpec((tokens, width), lambda h: (0, h)),
        out_shape=jax.ShapeDtypeStruct((tokens, heads * width), kind),
        interpret=interpret,
    )(local, rows, mask, state)


def shards(queries, keys, values, out_grad, gain, doc_ids):
    tokens_here = queries.shape[0]
    heads_here = queries.shape[1] // HD
    width_all = HEADS * HD
    flat_width = heads_here * HD
    query_heads = queries.reshape(tokens_here, heads_here, HD).transpose(1, 0, 2)
    key_heads = keys.reshape(tokens_here, heads_here, HD).transpose(1, 0, 2)
    value_heads = values.reshape(tokens_here, heads_here, HD).transpose(1, 0, 2)
    position = jnp.arange(tokens_here)
    doc_mask = (
        (doc_ids[:, None] == doc_ids[None, :]) & (position[:, None] >= position[None, :])
    ).astype(jnp.bfloat16)
    first_doc = doc_ids[0]
    last_doc = doc_ids[tokens_here - 1]
    first_tag = first_doc.astype(jnp.float32) + 1.0
    last_tag = last_doc.astype(jnp.float32) + 1.0
    first_mask = (doc_ids == first_doc).astype(jnp.bfloat16)[:, None]
    last_mask = (doc_ids == last_doc).astype(jnp.bfloat16)[:, None]
    first_rows = first_mask[None]
    last_rows = last_mask[None]
    query_first = query_heads * first_rows
    key_last = key_heads * last_rows
    own_state = jnp.einsum(
        "hta,htb->hab", key_last, value_heads, preferred_element_type=jnp.float32
    ).astype(jnp.bfloat16)
    incoming = carried(own_state, first_tag, last_tag, tokens_here, "ctx", False, jnp.bfloat16)
    scores = (
        jnp.einsum("hta,hsa->hts", query_heads, key_heads, preferred_element_type=jnp.float32)
        * doc_mask[None]
    ).astype(jnp.bfloat16)
    attended_local = jnp.einsum(
        "hts,hsb->htb", scores, value_heads, preferred_element_type=jnp.float32
    )
    flat = finished(attended_local, queries, first_mask, incoming, False, jnp.float32)
    scaled_grad = gain[None, :] * out_grad.astype(jnp.float32)
    sums = group_sum(
        jnp.stack([jnp.sum(flat * flat, axis=1), jnp.sum(scaled_grad * flat, axis=1)]), "tp"
    )
    square_sum, cross_sum = sums[0], sums[1]
    inverse = lax.rsqrt(square_sum / width_all + NORM_EPS)
    normed = (flat * inverse[:, None] * gain[None, :]).astype(jnp.bfloat16)
    delta = (
        inverse[:, None] * scaled_grad - flat * (inverse**3 * cross_sum / width_all)[:, None]
    ).astype(jnp.bfloat16)
    delta_heads = delta.reshape(tokens_here, heads_here, HD).transpose(1, 0, 2)
    own_reverse = jnp.einsum(
        "hta,htb->hab", query_first, delta_heads, preferred_element_type=jnp.float32
    ).astype(jnp.bfloat16)
    outgoing = carried(own_reverse, first_tag, last_tag, tokens_here, "ctx", True, jnp.bfloat16)
    dscores = (
        jnp.einsum("htb,hsb->hts", delta_heads, value_heads, preferred_element_type=jnp.float32)
        * doc_mask[None]
    ).astype(jnp.bfloat16)
    grad_query = jnp.einsum(
        "hts,hsa->hta", dscores, key_heads, preferred_element_type=jnp.float32
    )
    grad_key = jnp.einsum("hts,hta->hsa", dscores, query_heads, preferred_element_type=jnp.float32)
    grad_value = jnp.einsum("hts,htb->hsb", scores, delta_heads, preferred_element_type=jnp.float32)
    return (
        normed,
        finished(grad_query, delta, first_mask, incoming, True, jnp.bfloat16),
        finished(grad_key, values, last_mask, outgoing, True, jnp.bfloat16),
        finished(grad_value, keys, last_mask, outgoing, False, jnp.bfloat16),
    )


def solution(mesh):
    in_specs = (P("ctx", "tp"), P("ctx", "tp"), P("ctx", "tp"), P("ctx", "tp"), P("tp"), P("ctx"))
    out_specs = (P("ctx", "tp"), P("ctx", "tp"), P("ctx", "tp"), P("ctx", "tp"))
    return jax.shard_map(shards, mesh=mesh, in_specs=in_specs, out_specs=out_specs, check_vma=False)
```

```python
import jax
import jax.numpy as jnp
from jax import lax
from jax.experimental import pallas as pl
from jax.sharding import PartitionSpec as P

HEADS = 64
HD = 128
DOC_MOST = 12288

NORM_EPS = 1e-06


def moved(x, axis, count, by, backward):
    if backward:
        pairs = [(i, i - by) for i in range(by, count)]
    else:
        pairs = [(i, i + by) for i in range(count - by)]
    return lax.ppermute(x, axis, pairs)


def swapped(x, axis, count):
    return lax.ppermute(x, axis, [(i, i ^ 1) for i in range(count)])


def packed(data, tags):
    rows = data.reshape(-1, data.shape[-1])
    tail = jnp.zeros((16, rows.shape[1]), data.dtype)
    tail = tail.at[0, : len(tags)].set(jnp.stack(tags).astype(data.dtype))
    return jnp.concatenate([rows, tail], axis=0)


def unpacked(message, shape):
    data = message[: message.shape[0] - 16].reshape(shape)
    return data, message[message.shape[0] - 16, :4].astype(jnp.float32)


def carried(state, first_tag, last_tag, tokens_here, axis, backward, partial_type):
    count = lax.axis_size(axis)
    index = lax.axis_index(axis)
    if backward:
        link_tag, meet_tag, place = first_tag, last_tag, count - 1 - index
    else:
        link_tag, meet_tag, place = last_tag, first_tag, index
    chips = count // 2
    terms = min((DOC_MOST - 1) // tokens_here + 1, count)
    window = min((terms + 1) // 2, chips)
    core = place % 2
    half = state.shape[0] // 2
    half_shape = (half,) + state.shape[1:]
    own_half = lax.dynamic_slice_in_dim(state, core * half, half, 0)
    other_half = lax.dynamic_slice_in_dim(state, (1 - core) * half, half, 0)
    partner_half, partner_tags = unpacked(
        swapped(packed(other_half, [link_tag, meet_tag]), axis, count), half_shape
    )
    first_core = core == 0
    low = jnp.where(first_core, own_half, partner_half).astype(jnp.float32)
    high = jnp.where(first_core, partner_half, own_half).astype(jnp.float32)
    low_link = jnp.where(first_core, link_tag, partner_tags[0])
    high_link = jnp.where(first_core, partner_tags[0], link_tag)
    low_meet = jnp.where(first_core, meet_tag, partner_tags[1])
    high_meet = jnp.where(first_core, partner_tags[1], meet_tag)
    chip_total = high + (low_link == high_link).astype(jnp.float32) * low
    total, near_tags = unpacked(
        moved(packed(chip_total, [high_link]), axis, count, 2, backward), half_shape
    )
    before = near_tags[0]
    span = 1
    while span < window:
        far, far_tags = unpacked(
            moved(packed(total.astype(partial_type), [before]), axis, count, 2 * span, backward),
            half_shape,
        )
        reach = (far_tags[0] == before).astype(jnp.float32)
        total = total + reach * far.astype(jnp.float32)
        span = span * 2
    out_low = (before == low_meet).astype(jnp.float32) * total
    out_high = (low_link == high_meet).astype(jnp.float32) * (
        low + (before == low_link).astype(jnp.float32) * total
    )
    mine = jnp.where(first_core, out_low, out_high).astype(jnp.bfloat16)
    theirs = jnp.where(first_core, out_high, out_low).astype(jnp.bfloat16)
    got = swapped(theirs, axis, count)
    return jnp.where(
        first_core, jnp.concatenate([mine, got], axis=0), jnp.concatenate([got, mine], axis=0)
    )


def group_sum(x, axis):
    count = lax.axis_size(axis)
    step = 1
    while step < count:
        x = x + lax.ppermute(x, axis, [(i, i ^ step) for i in range(count)])
        step = step * 2
    return x


def finish_body(local_ref, rows_ref, mask_ref, state_ref, out_ref, *, flip):
    width = local_ref.shape[2]
    mask = mask_ref[...]
    for head in range(local_ref.shape[0]):
        cols = slice(head * width, (head + 1) * width)
        rows = rows_ref[:, cols] * mask
        state = state_ref[head]
        if flip:
            extra = lax.dot_general(
                rows, state, (((1,), (1,)), ((), ())), preferred_element_type=jnp.float32
            )
        else:
            extra = jnp.dot(rows, state, preferred_element_type=jnp.float32)
        out_ref[:, cols] = (local_ref[head] + extra).astype(out_ref.dtype)


def finished(local, rows, mask, state, flip, kind, interpret=False):
    heads, tokens, width = local.shape
    block = 256 if tokens % 256 == 0 else tokens
    return pl.pallas_call(
        lambda *refs: finish_body(*refs, flip=flip),
        grid=(tokens // block,),
        in_specs=[
            pl.BlockSpec((heads, block, width), lambda t: (0, t, 0)),
            pl.BlockSpec((block, heads * width), lambda t: (t, 0)),
            pl.BlockSpec((block, 1), lambda t: (t, 0)),
            pl.BlockSpec((heads, width, width), lambda t: (0, 0, 0)),
        ],
        out_specs=pl.BlockSpec((block, heads * width), lambda t: (t, 0)),
        out_shape=jax.ShapeDtypeStruct((tokens, heads * width), kind),
        interpret=interpret,
    )(local, rows, mask, state)


def shards(queries, keys, values, out_grad, gain, doc_ids):
    tokens_here = queries.shape[0]
    heads_here = queries.shape[1] // HD
    width_all = HEADS * HD
    flat_width = heads_here * HD
    query_heads = queries.reshape(tokens_here, heads_here, HD).transpose(1, 0, 2)
    key_heads = keys.reshape(tokens_here, heads_here, HD).transpose(1, 0, 2)
    value_heads = values.reshape(tokens_here, heads_here, HD).transpose(1, 0, 2)
    position = jnp.arange(tokens_here)
    doc_mask = (
        (doc_ids[:, None] == doc_ids[None, :]) & (position[:, None] >= position[None, :])
    ).astype(jnp.bfloat16)
    first_doc = doc_ids[0]
    last_doc = doc_ids[tokens_here - 1]
    first_tag = first_doc.astype(jnp.float32) + 1.0
    last_tag = last_doc.astype(jnp.float32) + 1.0
    first_mask = (doc_ids == first_doc).astype(jnp.bfloat16)[:, None]
    last_mask = (doc_ids == last_doc).astype(jnp.bfloat16)[:, None]
    first_rows = first_mask[None]
    last_rows = last_mask[None]
    query_first = query_heads * first_rows
    key_last = key_heads * last_rows
    own_state = jnp.einsum(
        "hta,htb->hab", key_last, value_heads, preferred_element_type=jnp.float32
    ).astype(jnp.bfloat16)
    incoming = carried(own_state, first_tag, last_tag, tokens_here, "ctx", False, jnp.bfloat16)
    scores = (
        jnp.einsum("hta,hsa->hts", query_heads, key_heads, preferred_element_type=jnp.float32)
        * doc_mask[None]
    ).astype(jnp.bfloat16)
    attended_local = jnp.einsum(
        "hts,hsb->htb", scores, value_heads, preferred_element_type=jnp.float32
    )
    flat = finished(attended_local, queries, first_mask, incoming, False, jnp.float32)
    scaled_grad = gain[None, :] * out_grad.astype(jnp.float32)
    sums = group_sum(
        jnp.stack([jnp.sum(flat * flat, axis=1), jnp.sum(scaled_grad * flat, axis=1)]), "tp"
    )
    square_sum, cross_sum = sums[0], sums[1]
    inverse = lax.rsqrt(square_sum / width_all + NORM_EPS)
    normed = (flat * inverse[:, None] * gain[None, :]).astype(jnp.bfloat16)
    delta = (
        inverse[:, None] * scaled_grad - flat * (inverse**3 * cross_sum / width_all)[:, None]
    ).astype(jnp.bfloat16)
    delta_heads = delta.reshape(tokens_here, heads_here, HD).transpose(1, 0, 2)
    own_reverse = jnp.einsum(
        "hta,htb->hab", query_first, delta_heads, preferred_element_type=jnp.float32
    ).astype(jnp.bfloat16)
    outgoing = carried(own_reverse, first_tag, last_tag, tokens_here, "ctx", True, jnp.bfloat16)
    dscores = (
        jnp.einsum("htb,hsb->hts", delta_heads, value_heads, preferred_element_type=jnp.float32)
        * doc_mask[None]
    ).astype(jnp.bfloat16)
    grad_query = jnp.einsum(
        "hts,hsa->hta", dscores, key_heads, preferred_element_type=jnp.float32
    )
    grad_key = jnp.einsum("hts,hta->hsa", dscores, query_heads, preferred_element_type=jnp.float32)
    grad_value = jnp.einsum("hts,htb->hsb", scores, delta_heads, preferred_element_type=jnp.float32)
    return (
        normed,
        finished(grad_query, delta, first_mask, incoming, True, jnp.bfloat16),
        finished(grad_key, values, last_mask, outgoing, True, jnp.bfloat16),
        finished(grad_value, keys, last_mask, outgoing, False, jnp.bfloat16),
    )


def solution(mesh):
    in_specs = (P("ctx", "tp"), P("ctx", "tp"), P("ctx", "tp"), P("ctx", "tp"), P("tp"), P("ctx"))
    out_specs = (P("ctx", "tp"), P("ctx", "tp"), P("ctx", "tp"), P("ctx", "tp"))
    return jax.shard_map(shards, mesh=mesh, in_specs=in_specs, out_specs=out_specs, check_vma=False)
```

```python
import jax
import jax.numpy as jnp
from jax import lax
from jax.experimental import pallas as pl
from jax.sharding import PartitionSpec as P

HEADS = 64
HD = 128
DOC_MOST = 12288

NORM_EPS = 1e-06


def moved(x, axis, count, by, backward):
    if backward:
        pairs = [(i, i - by) for i in range(by, count)]
    else:
        pairs = [(i, i + by) for i in range(count - by)]
    return lax.ppermute(x, axis, pairs)


def swapped(x, axis, count):
    return lax.ppermute(x, axis, [(i, i ^ 1) for i in range(count)])


def packed(data, tags):
    rows = data.reshape(-1, data.shape[-1])
    tail = jnp.zeros((16, rows.shape[1]), data.dtype)
    tail = tail.at[0, : len(tags)].set(jnp.stack(tags).astype(data.dtype))
    return jnp.concatenate([rows, tail], axis=0)


def unpacked(message, shape):
    data = message[: message.shape[0] - 16].reshape(shape)
    return data, message[message.shape[0] - 16, :4].astype(jnp.float32)


def carried(state, first_tag, last_tag, tokens_here, axis, backward, partial_type):
    count = lax.axis_size(axis)
    if backward:
        link_tag, meet_tag = first_tag, last_tag
    else:
        link_tag, meet_tag = last_tag, first_tag
    window = min((DOC_MOST - 1) // tokens_here + 1, count)
    shape = state.shape
    total, near_tags = unpacked(moved(packed(state, [link_tag]), axis, count, 1, backward), shape)
    total = total.astype(jnp.float32)
    before = near_tags[0]
    span = 1
    while span < window:
        far, far_tags = unpacked(
            moved(packed(total.astype(partial_type), [before]), axis, count, span, backward), shape
        )
        reach = (far_tags[0] == before).astype(jnp.float32)
        total = total + reach * far.astype(jnp.float32)
        span = span * 2
    return ((before == meet_tag).astype(jnp.float32) * total).astype(jnp.bfloat16)


def group_sum(x, axis):
    count = lax.axis_size(axis)
    step = 1
    while step < count:
        x = x + lax.ppermute(x, axis, [(i, i ^ step) for i in range(count)])
        step = step * 2
    return x


def finish_body(local_ref, rows_ref, mask_ref, state_ref, out_ref, *, flip):
    width = local_ref.shape[2]
    mask = mask_ref[...]
    for head in range(local_ref.shape[0]):
        cols = slice(head * width, (head + 1) * width)
        rows = rows_ref[:, cols] * mask
        state = state_ref[head]
        if flip:
            extra = lax.dot_general(
                rows, state, (((1,), (1,)), ((), ())), preferred_element_type=jnp.float32
            )
        else:
            extra = jnp.dot(rows, state, preferred_element_type=jnp.float32)
        out_ref[:, cols] = (local_ref[head] + extra).astype(out_ref.dtype)


def finished(local, rows, mask, state, flip, kind, interpret=False):
    heads, tokens, width = local.shape
    block = 256 if tokens % 256 == 0 else tokens
    return pl.pallas_call(
        lambda *refs: finish_body(*refs, flip=flip),
        grid=(tokens // block,),
        in_specs=[
            pl.BlockSpec((heads, block, width), lambda t: (0, t, 0)),
            pl.BlockSpec((block, heads * width), lambda t: (t, 0)),
            pl.BlockSpec((block, 1), lambda t: (t, 0)),
            pl.BlockSpec((heads, width, width), lambda t: (0, 0, 0)),
        ],
        out_specs=pl.BlockSpec((block, heads * width), lambda t: (t, 0)),
        out_shape=jax.ShapeDtypeStruct((tokens, heads * width), kind),
        interpret=interpret,
    )(local, rows, mask, state)


def shards(queries, keys, values, out_grad, gain, doc_ids):
    tokens_here = queries.shape[0]
    heads_here = queries.shape[1] // HD
    width_all = HEADS * HD
    flat_width = heads_here * HD
    query_heads = queries.reshape(tokens_here, heads_here, HD).transpose(1, 0, 2)
    key_heads = keys.reshape(tokens_here, heads_here, HD).transpose(1, 0, 2)
    value_heads = values.reshape(tokens_here, heads_here, HD).transpose(1, 0, 2)
    position = jnp.arange(tokens_here)
    doc_mask = (
        (doc_ids[:, None] == doc_ids[None, :]) & (position[:, None] >= position[None, :])
    ).astype(jnp.bfloat16)
    first_doc = doc_ids[0]
    last_doc = doc_ids[tokens_here - 1]
    first_tag = first_doc.astype(jnp.float32) + 1.0
    last_tag = last_doc.astype(jnp.float32) + 1.0
    first_mask = (doc_ids == first_doc).astype(jnp.bfloat16)[:, None]
    last_mask = (doc_ids == last_doc).astype(jnp.bfloat16)[:, None]
    first_rows = first_mask[None]
    last_rows = last_mask[None]
    query_first = query_heads * first_rows
    key_last = key_heads * last_rows
    own_state = jnp.einsum(
        "hta,htb->hab", key_last, value_heads, preferred_element_type=jnp.float32
    ).astype(jnp.bfloat16)
    incoming = carried(own_state, first_tag, last_tag, tokens_here, "ctx", False, jnp.bfloat16)
    scores = (
        jnp.einsum("hta,hsa->hts", query_heads, key_heads, preferred_element_type=jnp.float32)
        * doc_mask[None]
    ).astype(jnp.bfloat16)
    attended_local = jnp.einsum(
        "hts,hsb->htb", scores, value_heads, preferred_element_type=jnp.float32
    )
    flat = finished(attended_local, queries, first_mask, incoming, False, jnp.float32)
    scaled_grad = gain[None, :] * out_grad.astype(jnp.float32)
    sums = group_sum(
        jnp.stack([jnp.sum(flat * flat, axis=1), jnp.sum(scaled_grad * flat, axis=1)]), "tp"
    )
    square_sum, cross_sum = sums[0], sums[1]
    inverse = lax.rsqrt(square_sum / width_all + NORM_EPS)
    normed = (flat * inverse[:, None] * gain[None, :]).astype(jnp.bfloat16)
    delta = (
        inverse[:, None] * scaled_grad - flat * (inverse**3 * cross_sum / width_all)[:, None]
    ).astype(jnp.bfloat16)
    delta_heads = delta.reshape(tokens_here, heads_here, HD).transpose(1, 0, 2)
    own_reverse = jnp.einsum(
        "hta,htb->hab", query_first, delta_heads, preferred_element_type=jnp.float32
    ).astype(jnp.bfloat16)
    outgoing = carried(own_reverse, first_tag, last_tag, tokens_here, "ctx", True, jnp.bfloat16)
    dscores = (
        jnp.einsum("htb,hsb->hts", delta_heads, value_heads, preferred_element_type=jnp.float32)
        * doc_mask[None]
    ).astype(jnp.bfloat16)
    grad_query = jnp.einsum(
        "hts,hsa->hta", dscores, key_heads, preferred_element_type=jnp.float32
    )
    grad_key = jnp.einsum("hts,hta->hsa", dscores, query_heads, preferred_element_type=jnp.float32)
    grad_value = jnp.einsum("hts,htb->hsb", scores, delta_heads, preferred_element_type=jnp.float32)
    return (
        normed,
        finished(grad_query, delta, first_mask, incoming, True, jnp.bfloat16),
        finished(grad_key, values, last_mask, outgoing, True, jnp.bfloat16),
        finished(grad_value, keys, last_mask, outgoing, False, jnp.bfloat16),
    )


def solution(mesh):
    in_specs = (P("ctx", "tp"), P("ctx", "tp"), P("ctx", "tp"), P("ctx", "tp"), P("tp"), P("ctx"))
    out_specs = (P("ctx", "tp"), P("ctx", "tp"), P("ctx", "tp"), P("ctx", "tp"))
    return jax.shard_map(shards, mesh=mesh, in_specs=in_specs, out_specs=out_specs, check_vma=False)
```

```python
import jax
import jax.numpy as jnp
from jax import lax
from jax.experimental import pallas as pl
from jax.sharding import PartitionSpec as P

HEADS = 64
HD = 128
DOC_MOST = 12288

NORM_EPS = 1e-06


def moved(x, axis, count, by, backward):
    if backward:
        pairs = [(i, i - by) for i in range(by, count)]
    else:
        pairs = [(i, i + by) for i in range(count - by)]
    return lax.ppermute(x, axis, pairs)


def swapped(x, axis, count):
    return lax.ppermute(x, axis, [(i, i ^ 1) for i in range(count)])


def packed(data, tags):
    rows = data.reshape(-1, data.shape[-1])
    tail = jnp.zeros((16, rows.shape[1]), data.dtype)
    tail = tail.at[0, : len(tags)].set(jnp.stack(tags).astype(data.dtype))
    return jnp.concatenate([rows, tail], axis=0)


def unpacked(message, shape):
    data = message[: message.shape[0] - 16].reshape(shape)
    return data, message[message.shape[0] - 16, :4].astype(jnp.float32)


def carried(state, first_tag, last_tag, tokens_here, axis, backward, partial_type):
    count = lax.axis_size(axis)
    if backward:
        link_tag, meet_tag = first_tag, last_tag
    else:
        link_tag, meet_tag = last_tag, first_tag
    window = min((DOC_MOST - 1) // tokens_here + 1, count)
    shape = state.shape
    message = packed(state, [link_tag])
    total, near_tags = unpacked(moved(message, axis, count, 1, backward), shape)
    total = total.astype(jnp.float32)
    before = near_tags[0]
    span = 1
    if window > 1:
        second, second_tags = unpacked(moved(message, axis, count, 2, backward), shape)
        total = total + (second_tags[0] == before).astype(jnp.float32) * second.astype(jnp.float32)
        span = 2
    while span < window:
        far, far_tags = unpacked(
            moved(packed(total.astype(partial_type), [before]), axis, count, span, backward), shape
        )
        reach = (far_tags[0] == before).astype(jnp.float32)
        total = total + reach * far.astype(jnp.float32)
        span = span * 2
    return ((before == meet_tag).astype(jnp.float32) * total).astype(jnp.bfloat16)


def group_sum(x, axis):
    count = lax.axis_size(axis)
    step = 1
    while step < count:
        x = x + lax.ppermute(x, axis, [(i, i ^ step) for i in range(count)])
        step = step * 2
    return x


def finish_body(local_ref, rows_ref, mask_ref, state_ref, out_ref, *, flip):
    width = local_ref.shape[2]
    mask = mask_ref[...]
    for head in range(local_ref.shape[0]):
        cols = slice(head * width, (head + 1) * width)
        rows = rows_ref[:, cols] * mask
        state = state_ref[head]
        if flip:
            extra = lax.dot_general(
                rows, state, (((1,), (1,)), ((), ())), preferred_element_type=jnp.float32
            )
        else:
            extra = jnp.dot(rows, state, preferred_element_type=jnp.float32)
        out_ref[:, cols] = (local_ref[head] + extra).astype(out_ref.dtype)


def finished(local, rows, mask, state, flip, kind, interpret=False):
    heads, tokens, width = local.shape
    block = 256 if tokens % 256 == 0 else tokens
    return pl.pallas_call(
        lambda *refs: finish_body(*refs, flip=flip),
        grid=(tokens // block,),
        in_specs=[
            pl.BlockSpec((heads, block, width), lambda t: (0, t, 0)),
            pl.BlockSpec((block, heads * width), lambda t: (t, 0)),
            pl.BlockSpec((block, 1), lambda t: (t, 0)),
            pl.BlockSpec((heads, width, width), lambda t: (0, 0, 0)),
        ],
        out_specs=pl.BlockSpec((block, heads * width), lambda t: (t, 0)),
        out_shape=jax.ShapeDtypeStruct((tokens, heads * width), kind),
        interpret=interpret,
    )(local, rows, mask, state)


def shards(queries, keys, values, out_grad, gain, doc_ids):
    tokens_here = queries.shape[0]
    heads_here = queries.shape[1] // HD
    width_all = HEADS * HD
    flat_width = heads_here * HD
    query_heads = queries.reshape(tokens_here, heads_here, HD).transpose(1, 0, 2)
    key_heads = keys.reshape(tokens_here, heads_here, HD).transpose(1, 0, 2)
    value_heads = values.reshape(tokens_here, heads_here, HD).transpose(1, 0, 2)
    position = jnp.arange(tokens_here)
    doc_mask = (
        (doc_ids[:, None] == doc_ids[None, :]) & (position[:, None] >= position[None, :])
    ).astype(jnp.bfloat16)
    first_doc = doc_ids[0]
    last_doc = doc_ids[tokens_here - 1]
    first_tag = first_doc.astype(jnp.float32) + 1.0
    last_tag = last_doc.astype(jnp.float32) + 1.0
    first_mask = (doc_ids == first_doc).astype(jnp.bfloat16)[:, None]
    last_mask = (doc_ids == last_doc).astype(jnp.bfloat16)[:, None]
    first_rows = first_mask[None]
    last_rows = last_mask[None]
    query_first = query_heads * first_rows
    key_last = key_heads * last_rows
    own_state = jnp.einsum(
        "hta,htb->hab", key_last, value_heads, preferred_element_type=jnp.float32
    ).astype(jnp.bfloat16)
    incoming = carried(own_state, first_tag, last_tag, tokens_here, "ctx", False, jnp.bfloat16)
    scores = (
        jnp.einsum("hta,hsa->hts", query_heads, key_heads, preferred_element_type=jnp.float32)
        * doc_mask[None]
    ).astype(jnp.bfloat16)
    attended_local = jnp.einsum(
        "hts,hsb->htb", scores, value_heads, preferred_element_type=jnp.float32
    )
    flat = finished(attended_local, queries, first_mask, incoming, False, jnp.float32)
    scaled_grad = gain[None, :] * out_grad.astype(jnp.float32)
    sums = group_sum(
        jnp.stack([jnp.sum(flat * flat, axis=1), jnp.sum(scaled_grad * flat, axis=1)]), "tp"
    )
    square_sum, cross_sum = sums[0], sums[1]
    inverse = lax.rsqrt(square_sum / width_all + NORM_EPS)
    normed = (flat * inverse[:, None] * gain[None, :]).astype(jnp.bfloat16)
    delta = (
        inverse[:, None] * scaled_grad - flat * (inverse**3 * cross_sum / width_all)[:, None]
    ).astype(jnp.bfloat16)
    delta_heads = delta.reshape(tokens_here, heads_here, HD).transpose(1, 0, 2)
    own_reverse = jnp.einsum(
        "hta,htb->hab", query_first, delta_heads, preferred_element_type=jnp.float32
    ).astype(jnp.bfloat16)
    outgoing = carried(own_reverse, first_tag, last_tag, tokens_here, "ctx", True, jnp.bfloat16)
    dscores = (
        jnp.einsum("htb,hsb->hts", delta_heads, value_heads, preferred_element_type=jnp.float32)
        * doc_mask[None]
    ).astype(jnp.bfloat16)
    grad_query = jnp.einsum(
        "hts,hsa->hta", dscores, key_heads, preferred_element_type=jnp.float32
    )
    grad_key = jnp.einsum("hts,hta->hsa", dscores, query_heads, preferred_element_type=jnp.float32)
    grad_value = jnp.einsum("hts,htb->hsb", scores, delta_heads, preferred_element_type=jnp.float32)
    return (
        normed,
        finished(grad_query, delta, first_mask, incoming, True, jnp.bfloat16),
        finished(grad_key, values, last_mask, outgoing, True, jnp.bfloat16),
        finished(grad_value, keys, last_mask, outgoing, False, jnp.bfloat16),
    )


def solution(mesh):
    in_specs = (P("ctx", "tp"), P("ctx", "tp"), P("ctx", "tp"), P("ctx", "tp"), P("tp"), P("ctx"))
    out_specs = (P("ctx", "tp"), P("ctx", "tp"), P("ctx", "tp"), P("ctx", "tp"))
    return jax.shard_map(shards, mesh=mesh, in_specs=in_specs, out_specs=out_specs, check_vma=False)
```

```python
import jax
import jax.numpy as jnp
from jax import lax
from jax.experimental import pallas as pl
from jax.sharding import PartitionSpec as P

HEADS = 64
HD = 128
DOC_MOST = 12288

NORM_EPS = 1e-06


def moved(x, axis, count, by, backward):
    if backward:
        pairs = [(i, i - by) for i in range(by, count)]
    else:
        pairs = [(i, i + by) for i in range(count - by)]
    return lax.ppermute(x, axis, pairs)


def swapped(x, axis, count):
    return lax.ppermute(x, axis, [(i, i ^ 1) for i in range(count)])


def packed(data, tags):
    rows = data.reshape(-1, data.shape[-1])
    tail = jnp.zeros((16, rows.shape[1]), data.dtype)
    tail = tail.at[0, : len(tags)].set(jnp.stack(tags).astype(data.dtype))
    return jnp.concatenate([rows, tail], axis=0)


def unpacked(message, shape):
    data = message[: message.shape[0] - 16].reshape(shape)
    return data, message[message.shape[0] - 16, :4].astype(jnp.float32)


def carried(state, first_tag, last_tag, tokens_here, axis, backward, partial_type):
    count = lax.axis_size(axis)
    if backward:
        link_tag, meet_tag = first_tag, last_tag
    else:
        link_tag, meet_tag = last_tag, first_tag
    window = min((DOC_MOST - 1) // tokens_here + 1, count)
    shape = state.shape
    message = packed(state, [link_tag])
    total, near_tags = unpacked(moved(message, axis, count, 1, backward), shape)
    total = total.astype(jnp.float32)
    before = near_tags[0]
    span = 1
    if window > 1:
        second, second_tags = unpacked(moved(message, axis, count, 2, backward), shape)
        total = total + (second_tags[0] == before).astype(jnp.float32) * second.astype(jnp.float32)
        span = 2
    while span < window:
        far, far_tags = unpacked(
            moved(packed(total.astype(partial_type), [before]), axis, count, span, backward), shape
        )
        reach = (far_tags[0] == before).astype(jnp.float32)
        total = total + reach * far.astype(jnp.float32)
        span = span * 2
    return ((before == meet_tag).astype(jnp.float32) * total).astype(jnp.bfloat16)


def group_sum(x, axis):
    count = lax.axis_size(axis)
    step = 1
    while step < count:
        x = x + lax.ppermute(x, axis, [(i, i ^ step) for i in range(count)])
        step = step * 2
    return x


def finish_body(*refs, flips):
    parts = len(flips)
    locals_, rows_, mask_ref, state_ref = refs[:parts], refs[parts : 2 * parts], refs[2 * parts], refs[2 * parts + 1]
    outs = refs[2 * parts + 2 :]
    width = locals_[0].shape[2]
    mask = mask_ref[...]
    for head in range(locals_[0].shape[0]):
        cols = slice(head * width, (head + 1) * width)
        state = state_ref[head]
        for local_ref, rows_ref, out_ref, flip in zip(locals_, rows_, outs, flips):
            rows = rows_ref[:, cols] * mask
            if flip:
                extra = lax.dot_general(
                    rows, state, (((1,), (1,)), ((), ())), preferred_element_type=jnp.float32
                )
            else:
                extra = jnp.dot(rows, state, preferred_element_type=jnp.float32)
            out_ref[:, cols] = (local_ref[head] + extra).astype(out_ref.dtype)


def finished_all(locals_, rows_, mask, state, flips, kinds, interpret=False):
    heads, tokens, width = locals_[0].shape
    block = 128 if tokens % 128 == 0 else tokens
    local_spec = pl.BlockSpec((heads, block, width), lambda t: (0, t, 0))
    row_spec = pl.BlockSpec((block, heads * width), lambda t: (t, 0))
    return pl.pallas_call(
        lambda *refs: finish_body(*refs, flips=flips),
        grid=(tokens // block,),
        in_specs=[local_spec] * len(flips)
        + [row_spec] * len(flips)
        + [
            pl.BlockSpec((block, 1), lambda t: (t, 0)),
            pl.BlockSpec((heads, width, width), lambda t: (0, 0, 0)),
        ],
        out_specs=[row_spec] * len(flips),
        out_shape=[jax.ShapeDtypeStruct((tokens, heads * width), kind) for kind in kinds],
        interpret=interpret,
    )(*locals_, *rows_, mask, state)


def finished(local, rows, mask, state, flip, kind, interpret=False):
    return finished_all([local], [rows], mask, state, (flip,), (kind,), interpret)[0]


def shards(queries, keys, values, out_grad, gain, doc_ids):
    tokens_here = queries.shape[0]
    heads_here = queries.shape[1] // HD
    width_all = HEADS * HD
    flat_width = heads_here * HD
    query_heads = queries.reshape(tokens_here, heads_here, HD).transpose(1, 0, 2)
    key_heads = keys.reshape(tokens_here, heads_here, HD).transpose(1, 0, 2)
    value_heads = values.reshape(tokens_here, heads_here, HD).transpose(1, 0, 2)
    position = jnp.arange(tokens_here)
    doc_mask = (
        (doc_ids[:, None] == doc_ids[None, :]) & (position[:, None] >= position[None, :])
    ).astype(jnp.bfloat16)
    first_doc = doc_ids[0]
    last_doc = doc_ids[tokens_here - 1]
    first_tag = first_doc.astype(jnp.float32) + 1.0
    last_tag = last_doc.astype(jnp.float32) + 1.0
    first_mask = (doc_ids == first_doc).astype(jnp.bfloat16)[:, None]
    last_mask = (doc_ids == last_doc).astype(jnp.bfloat16)[:, None]
    first_rows = first_mask[None]
    last_rows = last_mask[None]
    query_first = query_heads * first_rows
    key_last = key_heads * last_rows
    own_state = jnp.einsum(
        "hta,htb->hab", key_last, value_heads, preferred_element_type=jnp.float32
    ).astype(jnp.bfloat16)
    incoming = carried(own_state, first_tag, last_tag, tokens_here, "ctx", False, jnp.bfloat16)
    scores = (
        jnp.einsum("hta,hsa->hts", query_heads, key_heads, preferred_element_type=jnp.float32)
        * doc_mask[None]
    ).astype(jnp.bfloat16)
    attended_local = jnp.einsum(
        "hts,hsb->htb", scores, value_heads, preferred_element_type=jnp.float32
    )
    flat = finished(attended_local, queries, first_mask, incoming, False, jnp.float32)
    scaled_grad = gain[None, :] * out_grad.astype(jnp.float32)
    sums = group_sum(
        jnp.stack([jnp.sum(flat * flat, axis=1), jnp.sum(scaled_grad * flat, axis=1)]), "tp"
    )
    square_sum, cross_sum = sums[0], sums[1]
    inverse = lax.rsqrt(square_sum / width_all + NORM_EPS)
    normed = (flat * inverse[:, None] * gain[None, :]).astype(jnp.bfloat16)
    delta = (
        inverse[:, None] * scaled_grad - flat * (inverse**3 * cross_sum / width_all)[:, None]
    ).astype(jnp.bfloat16)
    delta_heads = delta.reshape(tokens_here, heads_here, HD).transpose(1, 0, 2)
    own_reverse = jnp.einsum(
        "hta,htb->hab", query_first, delta_heads, preferred_element_type=jnp.float32
    ).astype(jnp.bfloat16)
    outgoing = carried(own_reverse, first_tag, last_tag, tokens_here, "ctx", True, jnp.bfloat16)
    dscores = (
        jnp.einsum("htb,hsb->hts", delta_heads, value_heads, preferred_element_type=jnp.float32)
        * doc_mask[None]
    ).astype(jnp.bfloat16)
    grad_query = jnp.einsum(
        "hts,hsa->hta", dscores, key_heads, preferred_element_type=jnp.float32
    )
    grad_key = jnp.einsum("hts,hta->hsa", dscores, query_heads, preferred_element_type=jnp.float32)
    grad_value = jnp.einsum("hts,htb->hsb", scores, delta_heads, preferred_element_type=jnp.float32)
    return (
        normed,
        finished(grad_query, delta, first_mask, incoming, True, jnp.bfloat16),
        *finished_all(
            [grad_key, grad_value],
            [values, keys],
            last_mask,
            outgoing,
            (True, False),
            (jnp.bfloat16, jnp.bfloat16),
        ),
    )


def solution(mesh):
    in_specs = (P("ctx", "tp"), P("ctx", "tp"), P("ctx", "tp"), P("ctx", "tp"), P("tp"), P("ctx"))
    out_specs = (P("ctx", "tp"), P("ctx", "tp"), P("ctx", "tp"), P("ctx", "tp"))
    return jax.shard_map(shards, mesh=mesh, in_specs=in_specs, out_specs=out_specs, check_vma=False)
```

```python
import jax
import jax.numpy as jnp
from jax import lax
from jax.experimental import pallas as pl
from jax.sharding import PartitionSpec as P

HEADS = 64
HD = 128
DOC_MOST = 12288

NORM_EPS = 1e-06


def moved(x, axis, count, by, backward):
    if backward:
        pairs = [(i, i - by) for i in range(by, count)]
    else:
        pairs = [(i, i + by) for i in range(count - by)]
    return lax.ppermute(x, axis, pairs)


def swapped(x, axis, count):
    return lax.ppermute(x, axis, [(i, i ^ 1) for i in range(count)])


def packed(data, tags):
    rows = data.reshape(-1, data.shape[-1])
    tail = jnp.zeros((16, rows.shape[1]), data.dtype)
    tail = tail.at[0, : len(tags)].set(jnp.stack(tags).astype(data.dtype))
    return jnp.concatenate([rows, tail], axis=0)


def unpacked(message, shape):
    data = message[: message.shape[0] - 16].reshape(shape)
    return data, message[message.shape[0] - 16, :4].astype(jnp.float32)


def carried(state, first_tag, last_tag, tokens_here, axis, backward, partial_type):
    count = lax.axis_size(axis)
    if backward:
        link_tag, meet_tag = first_tag, last_tag
    else:
        link_tag, meet_tag = last_tag, first_tag
    window = min((DOC_MOST - 1) // tokens_here + 1, count)
    shape = state.shape
    message = packed(state, [link_tag])
    total, near_tags = unpacked(moved(message, axis, count, 1, backward), shape)
    total = total.astype(jnp.float32)
    before = near_tags[0]
    span = 1
    if window > 1:
        second, second_tags = unpacked(moved(message, axis, count, 2, backward), shape)
        total = total + (second_tags[0] == before).astype(jnp.float32) * second.astype(jnp.float32)
        span = 2
    while span < window:
        far, far_tags = unpacked(
            moved(packed(total.astype(partial_type), [before]), axis, count, span, backward), shape
        )
        reach = (far_tags[0] == before).astype(jnp.float32)
        total = total + reach * far.astype(jnp.float32)
        span = span * 2
    return ((before == meet_tag).astype(jnp.float32) * total).astype(jnp.bfloat16)


def group_sum(x, axis):
    count = lax.axis_size(axis)
    step = 1
    while step < count:
        x = x + lax.ppermute(x, axis, [(i, i ^ step) for i in range(count)])
        step = step * 2
    return x


def finish_body(*refs, flips):
    parts = len(flips)
    locals_, rows_, mask_ref, state_ref = refs[:parts], refs[parts : 2 * parts], refs[2 * parts], refs[2 * parts + 1]
    outs = refs[2 * parts + 2 :]
    width = locals_[0].shape[2]
    mask = mask_ref[...]
    for head in range(locals_[0].shape[0]):
        cols = slice(head * width, (head + 1) * width)
        state = state_ref[head]
        for local_ref, rows_ref, out_ref, flip in zip(locals_, rows_, outs, flips):
            rows = rows_ref[:, cols] * mask
            if flip:
                extra = lax.dot_general(
                    rows, state, (((1,), (1,)), ((), ())), preferred_element_type=jnp.float32
                )
            else:
                extra = jnp.dot(rows, state, preferred_element_type=jnp.float32)
            out_ref[:, cols] = (local_ref[head] + extra).astype(out_ref.dtype)


def finished_all(locals_, rows_, mask, state, flips, kinds, interpret=False):
    heads, tokens, width = locals_[0].shape
    size = 128 if len(flips) > 1 else 256
    block = size if tokens % size == 0 else tokens
    local_spec = pl.BlockSpec((heads, block, width), lambda t: (0, t, 0))
    row_spec = pl.BlockSpec((block, heads * width), lambda t: (t, 0))
    return pl.pallas_call(
        lambda *refs: finish_body(*refs, flips=flips),
        grid=(tokens // block,),
        in_specs=[local_spec] * len(flips)
        + [row_spec] * len(flips)
        + [
            pl.BlockSpec((block, 1), lambda t: (t, 0)),
            pl.BlockSpec((heads, width, width), lambda t: (0, 0, 0)),
        ],
        out_specs=[row_spec] * len(flips),
        out_shape=[jax.ShapeDtypeStruct((tokens, heads * width), kind) for kind in kinds],
        interpret=interpret,
    )(*locals_, *rows_, mask, state)


def finished(local, rows, mask, state, flip, kind, interpret=False):
    return finished_all([local], [rows], mask, state, (flip,), (kind,), interpret)[0]


def attend_body(local_ref, rows_ref, mask_ref, state_ref, grad_ref, gain_ref, out_ref, sums_ref):
    width = local_ref.shape[2]
    mask = mask_ref[...]
    square = jnp.zeros((local_ref.shape[1], 1), jnp.float32)
    cross = jnp.zeros((local_ref.shape[1], 1), jnp.float32)
    for head in range(local_ref.shape[0]):
        cols = slice(head * width, (head + 1) * width)
        rows = rows_ref[:, cols] * mask
        flat = local_ref[head] + jnp.dot(rows, state_ref[head], preferred_element_type=jnp.float32)
        out_ref[:, cols] = flat
        scaled = gain_ref[:, cols] * grad_ref[:, cols].astype(jnp.float32)
        square = square + jnp.sum(flat * flat, axis=1, keepdims=True)
        cross = cross + jnp.sum(scaled * flat, axis=1, keepdims=True)
    sums_ref[...] = jnp.concatenate([square, cross], axis=1)


def attended_with_sums(local, rows, mask, state, out_grad, gain, interpret=False):
    heads, tokens, width = local.shape
    block = 256 if tokens % 256 == 0 else tokens
    row_spec = pl.BlockSpec((block, heads * width), lambda t: (t, 0))
    return pl.pallas_call(
        attend_body,
        grid=(tokens // block,),
        in_specs=[
            pl.BlockSpec((heads, block, width), lambda t: (0, t, 0)),
            row_spec,
            pl.BlockSpec((block, 1), lambda t: (t, 0)),
            pl.BlockSpec((heads, width, width), lambda t: (0, 0, 0)),
            row_spec,
            pl.BlockSpec((1, heads * width), lambda t: (0, 0)),
        ],
        out_specs=[row_spec, pl.BlockSpec((block, 2), lambda t: (t, 0))],
        out_shape=[
            jax.ShapeDtypeStruct((tokens, heads * width), jnp.float32),
            jax.ShapeDtypeStruct((tokens, 2), jnp.float32),
        ],
        interpret=interpret,
    )(local, rows, mask, state, out_grad, gain[None, :])


def shards(queries, keys, values, out_grad, gain, doc_ids):
    tokens_here = queries.shape[0]
    heads_here = queries.shape[1] // HD
    width_all = HEADS * HD
    flat_width = heads_here * HD
    query_heads = queries.reshape(tokens_here, heads_here, HD).transpose(1, 0, 2)
    key_heads = keys.reshape(tokens_here, heads_here, HD).transpose(1, 0, 2)
    value_heads = values.reshape(tokens_here, heads_here, HD).transpose(1, 0, 2)
    position = jnp.arange(tokens_here)
    doc_mask = (
        (doc_ids[:, None] == doc_ids[None, :]) & (position[:, None] >= position[None, :])
    ).astype(jnp.bfloat16)
    first_doc = doc_ids[0]
    last_doc = doc_ids[tokens_here - 1]
    first_tag = first_doc.astype(jnp.float32) + 1.0
    last_tag = last_doc.astype(jnp.float32) + 1.0
    first_mask = (doc_ids == first_doc).astype(jnp.bfloat16)[:, None]
    last_mask = (doc_ids == last_doc).astype(jnp.bfloat16)[:, None]
    first_rows = first_mask[None]
    last_rows = last_mask[None]
    query_first = query_heads * first_rows
    key_last = key_heads * last_rows
    own_state = jnp.einsum(
        "hta,htb->hab", key_last, value_heads, preferred_element_type=jnp.float32
    ).astype(jnp.bfloat16)
    incoming = carried(own_state, first_tag, last_tag, tokens_here, "ctx", False, jnp.bfloat16)
    scores = (
        jnp.einsum("hta,hsa->hts", query_heads, key_heads, preferred_element_type=jnp.float32)
        * doc_mask[None]
    ).astype(jnp.bfloat16)
    attended_local = jnp.einsum(
        "hts,hsb->htb", scores, value_heads, preferred_element_type=jnp.float32
    )
    flat, row_sums = attended_with_sums(
        attended_local, queries, first_mask, incoming, out_grad, gain
    )
    scaled_grad = gain[None, :] * out_grad.astype(jnp.float32)
    sums = group_sum(row_sums, "tp")
    square_sum, cross_sum = sums[:, 0], sums[:, 1]
    inverse = lax.rsqrt(square_sum / width_all + NORM_EPS)
    normed = (flat * inverse[:, None] * gain[None, :]).astype(jnp.bfloat16)
    delta = (
        inverse[:, None] * scaled_grad - flat * (inverse**3 * cross_sum / width_all)[:, None]
    ).astype(jnp.bfloat16)
    delta_heads = delta.reshape(tokens_here, heads_here, HD).transpose(1, 0, 2)
    own_reverse = jnp.einsum(
        "hta,htb->hab", query_first, delta_heads, preferred_element_type=jnp.float32
    ).astype(jnp.bfloat16)
    outgoing = carried(own_reverse, first_tag, last_tag, tokens_here, "ctx", True, jnp.bfloat16)
    dscores = (
        jnp.einsum("htb,hsb->hts", delta_heads, value_heads, preferred_element_type=jnp.float32)
        * doc_mask[None]
    ).astype(jnp.bfloat16)
    grad_query = jnp.einsum(
        "hts,hsa->hta", dscores, key_heads, preferred_element_type=jnp.float32
    )
    grad_key = jnp.einsum("hts,hta->hsa", dscores, query_heads, preferred_element_type=jnp.float32)
    grad_value = jnp.einsum("hts,htb->hsb", scores, delta_heads, preferred_element_type=jnp.float32)
    return (
        normed,
        finished(grad_query, delta, first_mask, incoming, True, jnp.bfloat16),
        *finished_all(
            [grad_key, grad_value],
            [values, keys],
            last_mask,
            outgoing,
            (True, False),
            (jnp.bfloat16, jnp.bfloat16),
        ),
    )


def solution(mesh):
    in_specs = (P("ctx", "tp"), P("ctx", "tp"), P("ctx", "tp"), P("ctx", "tp"), P("tp"), P("ctx"))
    out_specs = (P("ctx", "tp"), P("ctx", "tp"), P("ctx", "tp"), P("ctx", "tp"))
    return jax.shard_map(shards, mesh=mesh, in_specs=in_specs, out_specs=out_specs, check_vma=False)
```

```python
import jax
import jax.numpy as jnp
from jax import lax
from jax.experimental import pallas as pl
from jax.sharding import PartitionSpec as P

HEADS = 64
HD = 128
DOC_MOST = 12288

NORM_EPS = 1e-06


def moved(x, axis, count, by, backward):
    if backward:
        pairs = [(i, i - by) for i in range(by, count)]
    else:
        pairs = [(i, i + by) for i in range(count - by)]
    return lax.ppermute(x, axis, pairs)


def swapped(x, axis, count):
    return lax.ppermute(x, axis, [(i, i ^ 1) for i in range(count)])


def packed(data, tags):
    rows = data.reshape(-1, data.shape[-1])
    tail = jnp.zeros((16, rows.shape[1]), data.dtype)
    tail = tail.at[0, : len(tags)].set(jnp.stack(tags).astype(data.dtype))
    return jnp.concatenate([rows, tail], axis=0)


def unpacked(message, shape):
    data = message[: message.shape[0] - 16].reshape(shape)
    return data, message[message.shape[0] - 16, :4].astype(jnp.float32)


def carried(state, first_tag, last_tag, tokens_here, axis, backward, partial_type):
    count = lax.axis_size(axis)
    if backward:
        link_tag, meet_tag = first_tag, last_tag
    else:
        link_tag, meet_tag = last_tag, first_tag
    window = min((DOC_MOST - 1) // tokens_here + 1, count)
    shape = state.shape
    message = packed(state, [link_tag])
    total, near_tags = unpacked(moved(message, axis, count, 1, backward), shape)
    total = total.astype(jnp.float32)
    before = near_tags[0]
    span = 1
    if window > 1:
        second, second_tags = unpacked(moved(message, axis, count, 2, backward), shape)
        total = total + (second_tags[0] == before).astype(jnp.float32) * second.astype(jnp.float32)
        span = 2
    while span < window:
        far, far_tags = unpacked(
            moved(packed(total.astype(partial_type), [before]), axis, count, span, backward), shape
        )
        reach = (far_tags[0] == before).astype(jnp.float32)
        total = total + reach * far.astype(jnp.float32)
        span = span * 2
    return ((before == meet_tag).astype(jnp.float32) * total).astype(jnp.bfloat16)


def group_sum(x, axis):
    count = lax.axis_size(axis)
    step = 1
    while step < count:
        x = x + lax.ppermute(x, axis, [(i, i ^ step) for i in range(count)])
        step = step * 2
    return x


def finish_body(*refs, flips):
    parts = len(flips)
    locals_, rows_, mask_ref, state_ref = refs[:parts], refs[parts : 2 * parts], refs[2 * parts], refs[2 * parts + 1]
    outs = refs[2 * parts + 2 :]
    width = locals_[0].shape[2]
    mask = mask_ref[...]
    for head in range(locals_[0].shape[0]):
        cols = slice(head * width, (head + 1) * width)
        state = state_ref[head]
        for local_ref, rows_ref, out_ref, flip in zip(locals_, rows_, outs, flips):
            rows = rows_ref[:, cols] * mask
            if flip:
                extra = lax.dot_general(
                    rows, state, (((1,), (1,)), ((), ())), preferred_element_type=jnp.float32
                )
            else:
                extra = jnp.dot(rows, state, preferred_element_type=jnp.float32)
            out_ref[:, cols] = (local_ref[head] + extra).astype(out_ref.dtype)


def finished_all(locals_, rows_, mask, state, flips, kinds, interpret=False):
    heads, tokens, width = locals_[0].shape
    size = 128 if len(flips) > 1 else 256
    block = size if tokens % size == 0 else tokens
    local_spec = pl.BlockSpec((heads, block, width), lambda t: (0, t, 0))
    row_spec = pl.BlockSpec((block, heads * width), lambda t: (t, 0))
    return pl.pallas_call(
        lambda *refs: finish_body(*refs, flips=flips),
        grid=(tokens // block,),
        in_specs=[local_spec] * len(flips)
        + [row_spec] * len(flips)
        + [
            pl.BlockSpec((block, 1), lambda t: (t, 0)),
            pl.BlockSpec((heads, width, width), lambda t: (0, 0, 0)),
        ],
        out_specs=[row_spec] * len(flips),
        out_shape=[jax.ShapeDtypeStruct((tokens, heads * width), kind) for kind in kinds],
        interpret=interpret,
    )(*locals_, *rows_, mask, state)


def finished(local, rows, mask, state, flip, kind, interpret=False):
    return finished_all([local], [rows], mask, state, (flip,), (kind,), interpret)[0]


def attend_body(local_ref, rows_ref, mask_ref, state_ref, grad_ref, gain_ref, out_ref, sums_ref):
    width = local_ref.shape[2]
    mask = mask_ref[...]
    square = jnp.zeros((local_ref.shape[1], 1), jnp.float32)
    cross = jnp.zeros((local_ref.shape[1], 1), jnp.float32)
    for head in range(local_ref.shape[0]):
        cols = slice(head * width, (head + 1) * width)
        rows = rows_ref[:, cols] * mask
        flat = local_ref[head] + jnp.dot(rows, state_ref[head], preferred_element_type=jnp.float32)
        out_ref[:, cols] = flat
        scaled = gain_ref[:, cols] * grad_ref[:, cols].astype(jnp.float32)
        square = square + jnp.sum(flat * flat, axis=1, keepdims=True)
        cross = cross + jnp.sum(scaled * flat, axis=1, keepdims=True)
    sums_ref[...] = jnp.concatenate([square, cross], axis=1)


def attended_with_sums(local, rows, mask, state, out_grad, gain, interpret=False):
    heads, tokens, width = local.shape
    block = 256 if tokens % 256 == 0 else tokens
    row_spec = pl.BlockSpec((block, heads * width), lambda t: (t, 0))
    return pl.pallas_call(
        attend_body,
        grid=(tokens // block,),
        in_specs=[
            pl.BlockSpec((heads, block, width), lambda t: (0, t, 0)),
            row_spec,
            pl.BlockSpec((block, 1), lambda t: (t, 0)),
            pl.BlockSpec((heads, width, width), lambda t: (0, 0, 0)),
            row_spec,
            pl.BlockSpec((1, heads * width), lambda t: (0, 0)),
        ],
        out_specs=[row_spec, pl.BlockSpec((block, 2), lambda t: (t, 0))],
        out_shape=[
            jax.ShapeDtypeStruct((tokens, heads * width), jnp.float32),
            jax.ShapeDtypeStruct((tokens, 2), jnp.float32),
        ],
        interpret=interpret,
    )(local, rows, mask, state, out_grad, gain[None, :])


def shards(queries, keys, values, out_grad, gain, doc_ids):
    tokens_here = queries.shape[0]
    heads_here = queries.shape[1] // HD
    width_all = HEADS * HD
    flat_width = heads_here * HD
    query_heads = queries.reshape(tokens_here, heads_here, HD).transpose(1, 0, 2)
    key_heads = keys.reshape(tokens_here, heads_here, HD).transpose(1, 0, 2)
    value_heads = values.reshape(tokens_here, heads_here, HD).transpose(1, 0, 2)
    position = jnp.arange(tokens_here)
    doc_mask = (
        (doc_ids[:, None] == doc_ids[None, :]) & (position[:, None] >= position[None, :])
    ).astype(jnp.bfloat16)
    first_doc = doc_ids[0]
    last_doc = doc_ids[tokens_here - 1]
    first_tag = first_doc.astype(jnp.float32) + 1.0
    last_tag = last_doc.astype(jnp.float32) + 1.0
    first_mask = (doc_ids == first_doc).astype(jnp.bfloat16)[:, None]
    last_mask = (doc_ids == last_doc).astype(jnp.bfloat16)[:, None]
    first_rows = first_mask[None]
    last_rows = last_mask[None]
    query_first = query_heads * first_rows
    key_last = key_heads * last_rows
    own_state = jnp.einsum(
        "hta,htb->hab", key_last, value_heads, preferred_element_type=jnp.float32
    ).astype(jnp.bfloat16)
    incoming = carried(own_state, first_tag, last_tag, tokens_here, "ctx", False, jnp.bfloat16)
    scores = (
        jnp.einsum("hta,hsa->hts", query_heads, key_heads, preferred_element_type=jnp.float32)
        * doc_mask[None]
    ).astype(jnp.bfloat16)
    attended_local = jnp.einsum(
        "hts,hsb->htb", scores, value_heads, preferred_element_type=jnp.float32
    )
    flat, row_sums = attended_with_sums(
        attended_local, queries, first_mask, incoming, out_grad, gain
    )
    scaled_grad = gain[None, :] * out_grad.astype(jnp.float32)
    sums = group_sum(row_sums.T, "tp")
    square_sum, cross_sum = sums[0], sums[1]
    inverse = lax.rsqrt(square_sum / width_all + NORM_EPS)
    normed = (flat * inverse[:, None] * gain[None, :]).astype(jnp.bfloat16)
    delta = (
        inverse[:, None] * scaled_grad - flat * (inverse**3 * cross_sum / width_all)[:, None]
    ).astype(jnp.bfloat16)
    delta_heads = delta.reshape(tokens_here, heads_here, HD).transpose(1, 0, 2)
    own_reverse = jnp.einsum(
        "hta,htb->hab", query_first, delta_heads, preferred_element_type=jnp.float32
    ).astype(jnp.bfloat16)
    outgoing = carried(own_reverse, first_tag, last_tag, tokens_here, "ctx", True, jnp.bfloat16)
    dscores = (
        jnp.einsum("htb,hsb->hts", delta_heads, value_heads, preferred_element_type=jnp.float32)
        * doc_mask[None]
    ).astype(jnp.bfloat16)
    grad_query = jnp.einsum(
        "hts,hsa->hta", dscores, key_heads, preferred_element_type=jnp.float32
    )
    grad_key = jnp.einsum("hts,hta->hsa", dscores, query_heads, preferred_element_type=jnp.float32)
    grad_value = jnp.einsum("hts,htb->hsb", scores, delta_heads, preferred_element_type=jnp.float32)
    return (
        normed,
        finished(grad_query, delta, first_mask, incoming, True, jnp.bfloat16),
        *finished_all(
            [grad_key, grad_value],
            [values, keys],
            last_mask,
            outgoing,
            (True, False),
            (jnp.bfloat16, jnp.bfloat16),
        ),
    )


def solution(mesh):
    in_specs = (P("ctx", "tp"), P("ctx", "tp"), P("ctx", "tp"), P("ctx", "tp"), P("tp"), P("ctx"))
    out_specs = (P("ctx", "tp"), P("ctx", "tp"), P("ctx", "tp"), P("ctx", "tp"))
    return jax.shard_map(shards, mesh=mesh, in_specs=in_specs, out_specs=out_specs, check_vma=False)
```

```python
import jax
import jax.numpy as jnp
from jax import lax
from jax.experimental import pallas as pl
from jax.sharding import PartitionSpec as P

HEADS = 64
HD = 128
DOC_MOST = 12288

NORM_EPS = 1e-06


def moved(x, axis, count, by, backward):
    if backward:
        pairs = [(i, i - by) for i in range(by, count)]
    else:
        pairs = [(i, i + by) for i in range(count - by)]
    return lax.ppermute(x, axis, pairs)


def swapped(x, axis, count):
    return lax.ppermute(x, axis, [(i, i ^ 1) for i in range(count)])


def packed(data, tags):
    rows = data.reshape(-1, data.shape[-1])
    tail = jnp.zeros((16, rows.shape[1]), data.dtype)
    tail = tail.at[0, : len(tags)].set(jnp.stack(tags).astype(data.dtype))
    return jnp.concatenate([rows, tail], axis=0)


def unpacked(message, shape):
    data = message[: message.shape[0] - 16].reshape(shape)
    return data, message[message.shape[0] - 16, :4].astype(jnp.float32)


def carried(state, first_tag, last_tag, tokens_here, axis, backward, partial_type):
    count = lax.axis_size(axis)
    if backward:
        link_tag, meet_tag = first_tag, last_tag
    else:
        link_tag, meet_tag = last_tag, first_tag
    window = min((DOC_MOST - 1) // tokens_here + 1, count)
    shape = state.shape
    message = packed(state, [link_tag])
    total, near_tags = unpacked(moved(message, axis, count, 1, backward), shape)
    total = total.astype(jnp.float32)
    before = near_tags[0]
    span = 1
    if window > 1:
        second, second_tags = unpacked(moved(message, axis, count, 2, backward), shape)
        total = total + (second_tags[0] == before).astype(jnp.float32) * second.astype(jnp.float32)
        span = 2
    while span < window:
        far, far_tags = unpacked(
            moved(packed(total.astype(partial_type), [before]), axis, count, span, backward), shape
        )
        reach = (far_tags[0] == before).astype(jnp.float32)
        total = total + reach * far.astype(jnp.float32)
        span = span * 2
    return ((before == meet_tag).astype(jnp.float32) * total).astype(jnp.bfloat16)


def group_sum(x, axis):
    count = lax.axis_size(axis)
    step = 1
    while step < count:
        x = x + lax.ppermute(x, axis, [(i, i ^ step) for i in range(count)])
        step = step * 2
    return x


def finish_body(*refs, flips):
    parts = len(flips)
    locals_, rows_, mask_ref, state_ref = refs[:parts], refs[parts : 2 * parts], refs[2 * parts], refs[2 * parts + 1]
    outs = refs[2 * parts + 2 :]
    width = locals_[0].shape[2]
    mask = mask_ref[...]
    for head in range(locals_[0].shape[0]):
        cols = slice(head * width, (head + 1) * width)
        state = state_ref[head]
        for local_ref, rows_ref, out_ref, flip in zip(locals_, rows_, outs, flips):
            rows = rows_ref[:, cols] * mask
            if flip:
                extra = lax.dot_general(
                    rows, state, (((1,), (1,)), ((), ())), preferred_element_type=jnp.float32
                )
            else:
                extra = jnp.dot(rows, state, preferred_element_type=jnp.float32)
            out_ref[:, cols] = (local_ref[head] + extra).astype(out_ref.dtype)


def finished_all(locals_, rows_, mask, state, flips, kinds, interpret=False):
    heads, tokens, width = locals_[0].shape
    size = 128 if len(flips) > 1 else 256
    block = size if tokens % size == 0 else tokens
    local_spec = pl.BlockSpec((heads, block, width), lambda t: (0, t, 0))
    row_spec = pl.BlockSpec((block, heads * width), lambda t: (t, 0))
    return pl.pallas_call(
        lambda *refs: finish_body(*refs, flips=flips),
        grid=(tokens // block,),
        in_specs=[local_spec] * len(flips)
        + [row_spec] * len(flips)
        + [
            pl.BlockSpec((block, 1), lambda t: (t, 0)),
            pl.BlockSpec((heads, width, width), lambda t: (0, 0, 0)),
        ],
        out_specs=[row_spec] * len(flips),
        out_shape=[jax.ShapeDtypeStruct((tokens, heads * width), kind) for kind in kinds],
        interpret=interpret,
    )(*locals_, *rows_, mask, state)


def finished(local, rows, mask, state, flip, kind, interpret=False):
    return finished_all([local], [rows], mask, state, (flip,), (kind,), interpret)[0]


def shards(queries, keys, values, out_grad, gain, doc_ids):
    tokens_here = queries.shape[0]
    heads_here = queries.shape[1] // HD
    width_all = HEADS * HD
    flat_width = heads_here * HD
    query_heads = queries.reshape(tokens_here, heads_here, HD).transpose(1, 0, 2)
    key_heads = keys.reshape(tokens_here, heads_here, HD).transpose(1, 0, 2)
    value_heads = values.reshape(tokens_here, heads_here, HD).transpose(1, 0, 2)
    position = jnp.arange(tokens_here)
    doc_mask = (
        (doc_ids[:, None] == doc_ids[None, :]) & (position[:, None] >= position[None, :])
    ).astype(jnp.bfloat16)
    first_doc = doc_ids[0]
    last_doc = doc_ids[tokens_here - 1]
    first_tag = first_doc.astype(jnp.float32) + 1.0
    last_tag = last_doc.astype(jnp.float32) + 1.0
    first_mask = (doc_ids == first_doc).astype(jnp.bfloat16)[:, None]
    last_mask = (doc_ids == last_doc).astype(jnp.bfloat16)[:, None]
    first_rows = first_mask[None]
    last_rows = last_mask[None]
    query_first = query_heads * first_rows
    key_last = key_heads * last_rows
    own_state = jnp.einsum(
        "hta,htb->hab", key_last, value_heads, preferred_element_type=jnp.float32
    ).astype(jnp.bfloat16)
    incoming = carried(own_state, first_tag, last_tag, tokens_here, "ctx", False, jnp.bfloat16)
    scores = (
        jnp.einsum("hta,hsa->hts", query_heads, key_heads, preferred_element_type=jnp.float32)
        * doc_mask[None]
    ).astype(jnp.bfloat16)
    attended_local = jnp.einsum(
        "hts,hsb->htb", scores, value_heads, preferred_element_type=jnp.float32
    )
    flat = finished(attended_local, queries, first_mask, incoming, False, jnp.float32)
    scaled_grad = gain[None, :] * out_grad.astype(jnp.float32)
    sums = group_sum(
        jnp.stack([jnp.sum(flat * flat, axis=1), jnp.sum(scaled_grad * flat, axis=1)]), "tp"
    )
    square_sum, cross_sum = sums[0], sums[1]
    inverse = lax.rsqrt(square_sum / width_all + NORM_EPS)
    normed = (flat * inverse[:, None] * gain[None, :]).astype(jnp.bfloat16)
    delta = (
        inverse[:, None] * scaled_grad - flat * (inverse**3 * cross_sum / width_all)[:, None]
    ).astype(jnp.bfloat16)
    delta_heads = delta.reshape(tokens_here, heads_here, HD).transpose(1, 0, 2)
    own_reverse = jnp.einsum(
        "hta,htb->hab", query_first, delta_heads, preferred_element_type=jnp.float32
    ).astype(jnp.bfloat16)
    outgoing = carried(own_reverse, first_tag, last_tag, tokens_here, "ctx", True, jnp.bfloat16)
    dscores = (
        jnp.einsum("htb,hsb->hts", delta_heads, value_heads, preferred_element_type=jnp.float32)
        * doc_mask[None]
    ).astype(jnp.bfloat16)
    grad_query = jnp.einsum(
        "hts,hsa->hta", dscores, key_heads, preferred_element_type=jnp.float32
    )
    grad_key = jnp.einsum("hts,hta->hsa", dscores, query_heads, preferred_element_type=jnp.float32)
    grad_value = jnp.einsum("hts,htb->hsb", scores, delta_heads, preferred_element_type=jnp.float32)
    return (
        normed,
        finished(grad_query, delta, first_mask, incoming, True, jnp.bfloat16),
        *finished_all(
            [grad_key, grad_value],
            [values, keys],
            last_mask,
            outgoing,
            (True, False),
            (jnp.bfloat16, jnp.bfloat16),
        ),
    )


def solution(mesh):
    in_specs = (P("ctx", "tp"), P("ctx", "tp"), P("ctx", "tp"), P("ctx", "tp"), P("tp"), P("ctx"))
    out_specs = (P("ctx", "tp"), P("ctx", "tp"), P("ctx", "tp"), P("ctx", "tp"))
    return jax.shard_map(shards, mesh=mesh, in_specs=in_specs, out_specs=out_specs, check_vma=False)
```
